256 devices in a mesh: dp: 64 (over y_hi, z, x), mp: 4 (over y_lo, core).
Axes of the slice: x: 4, y: 4 (y_hi: 2, y_lo: 2; y = y_hi * 2 + y_lo), z: 8, core: 2. Of those that a mesh axis runs over, the one named last changes fastest.
Arguments:
- image_feats: bfloat16 [65536, 1152], P('dp'), may hold values from -16 to 16
- text_feats: bfloat16 [65536, 1152], P('dp'), may hold values from -16 to 16
- image_head: bfloat16 [1152, 1152], P(None, 'mp')
- text_head: bfloat16 [1152, 1152], P(None, 'mp')
- hard_tiles: int32 [512, 16], P('dp'), may hold values from 0 to 511, as said below
- logit_scale: float32 [1], replicated, may hold values from 6 to 16
- logit_bias: float32 [1], replicated, may hold values from -4 to -1
Outputs:
- head_grad_img: float32 [1152, 1152], P('dp', 'mp')
- head_grad_txt: float32 [1152, 1152], P('dp', 'mp')
The draws below stay inside these ranges and needn't reach their ends.
Inputs may be any that keep to these rules, and one draw needn't show every extreme that they name: `hard_tiles`: row tile g lies in block i = g // 8; with o running over -2 .. -1, 1 .. 2 in order as o_0 .. o_(3), entries 4 * k to 4 * k + 3 of row g are 4 different tiles of block (i + o_k) mod 64, and block j holds tiles 8 * j to 8 * j + 7.
All inputs are finite; a program needn't handle non-finite values.
Results may differ from the reference program's by a relative error of at most 0.0015.
Values may be sent and summed in bfloat16 or wider, within the bound.
No kernel may reach another device: no remote copies, remote signals or barrier semaphores. Data moves between devices by JAX's collectives and lax.ppermute only.
A program may use at most 128 MiB of HBM per device.

```python
import math
import jax
import jax.numpy as jnp
from jax import lax

D = 1152
E = 1152
ROWS = 1024
TILE = 128
PICKS = 4
REACH = 2
HARD = 16
BLOCKS = 64
TILES_BLK = 8
PAIRS = 65536
NTILES = 512


def head_draw(key, salt):
    base_key = jax.random.fold_in(key, salt)
    entry_key = jax.random.fold_in(base_key, 1)
    column_key = jax.random.fold_in(base_key, 2)
    position = jnp.arange(E, dtype=jnp.float32) / (E - 1)
    base = jnp.clip(jax.random.normal(entry_key, (D, E), jnp.float32), -6.0, 6.0)
    rising = 3.0 ** (0.5 * position)
    spread = 10.0 ** jax.random.uniform(column_key, (E,), jnp.float32)
    return base * (spread * rising)[None, :] / math.sqrt(D)


def draw_image_head(key, part):
    return head_draw(key, 11).astype(jnp.bfloat16)


def draw_text_head(key, part):
    return head_draw(key, 23).astype(jnp.bfloat16)


def draw_hard_tiles(key, part):
    order_key = jax.random.fold_in(key, 101)
    ranking = jax.random.randint(order_key, (NTILES, 2 * REACH, TILES_BLK), 0, 1048576) * TILES_BLK
    ranking = ranking + jnp.arange(TILES_BLK, dtype=jnp.int32)[None, None, :]
    picked = jnp.argsort(ranking, axis=-1, stable=True)[:, :, :PICKS].astype(jnp.int32)
    offsets = jnp.concatenate([jnp.arange(-REACH, 0), jnp.arange(1, REACH + 1)]).astype(jnp.int32)
    home_block = jnp.arange(NTILES, dtype=jnp.int32) // TILES_BLK
    target = (home_block[:, None] + offsets[None, :]) % BLOCKS
    return (target[:, :, None] * TILES_BLK + picked).reshape(NTILES, HARD).astype(jnp.int32)


def with_spikes(result, key, source, target, parts, factor):
    def block_of(dim):
        return (jnp.arange(result.shape[dim]) // (result.shape[dim] // parts)).reshape((-1,) + (1,) * (result.ndim - 1 - dim))

    near = jax.random.permutation(key, parts)[block_of(target)]
    second = (block_of(target) + parts // 2) % parts
    return jnp.where((block_of(source) == near) | (block_of(source) == second), factor * result, result)


def levels(key, dims, pieces, least, top_value):
    level, own = 1.0, jax.random.fold_in(key, 6)
    for axis_at, blocks in pieces:
        heights = jnp.exp(jax.random.uniform(jax.random.fold_in(own, axis_at), (blocks,), jnp.float32, least / len(pieces), top_value / len(pieces)))
        level = level * jnp.repeat(heights, dims[axis_at] // blocks).reshape([-1 if axis == axis_at else 1 for axis in range(len(dims))])
    return level


def heavy_noise(key, extent, width, most, pieces, heavy, kind=jnp.bfloat16):
    result = width * jax.random.normal(key, extent, jnp.float32)
    if pieces:
        result = result * levels(key, extent, pieces, -0.22, 0.18)
    return jnp.clip(with_spikes(result, jax.random.fold_in(key, 3), *heavy), -most, most).astype(kind)


def setup_inputs(seed: int = 0) -> dict:
    splits = jax.random.split(jax.random.key(seed), 8)
    return {
        "image_feats": heavy_noise(splits[0], (PAIRS, D), 1.0, 16.0, ((0, 64),), (0, 1, 64, 4.0)),
        "text_feats": heavy_noise(splits[1], (PAIRS, D), 1.0, 16.0, ((0, 64),), (0, 1, 64, 4.0)),
        "image_head": draw_image_head(jax.random.fold_in(splits[7], 71), 0),
        "text_head": draw_text_head(jax.random.fold_in(splits[7], 71), 0),
        "hard_tiles": draw_hard_tiles(jax.random.fold_in(splits[7], 71), 0),
        "logit_scale": jnp.clip(jax.random.uniform(splits[5], (1,), jnp.float32, 6.0, 16.0), 6.0, 16.0),
        "logit_bias": jnp.clip(jax.random.uniform(splits[6], (1,), jnp.float32, -4.0, -1.0), -4.0, -1.0),
    }


EPSILON = 1e-06

def embed(features, head):
    projected = jnp.dot(features, head, preferred_element_type=jnp.float32)
    inverse = lax.rsqrt(lax.optimization_barrier(jnp.sum(projected * projected, axis=1)) + EPSILON)
    unit = (projected * inverse[:, None]).astype(jnp.bfloat16)
    return (projected, inverse, unit)

def reference(image_feats, text_feats, image_head, text_head, hard_tiles, logit_scale, logit_bias):
    temp_scale = logit_scale[0]
    shift_bias = logit_bias[0]
    proj_img, inv_img, unit_img = embed(image_feats, image_head)
    proj_txt, inv_txt, unit_txt = embed(text_feats, text_head)
    text_tiles = unit_txt.reshape(NTILES, TILE, E)
    hard_blocks = hard_tiles.reshape(BLOCKS, TILES_BLK, HARD)
    diagonal_mask = jnp.eye(ROWS, dtype=jnp.float32)

    def one_block(carried, block_index):
        start = (block_index * ROWS).astype(jnp.int32)
        image_rows = lax.dynamic_slice_in_dim(unit_img, start, ROWS, 0)
        text_rows = lax.dynamic_slice_in_dim(unit_txt, start, ROWS, 0)
        scores = jnp.dot(image_rows, text_rows.T, preferred_element_type=jnp.float32)
        weight = (temp_scale * (jax.nn.sigmoid(temp_scale * scores + shift_bias) - diagonal_mask)).astype(jnp.bfloat16)
        grad_rows = jnp.dot(weight, text_rows, preferred_element_type=jnp.float32)
        grad_own = jnp.dot(weight.T, image_rows, preferred_element_type=jnp.float32)
        listed = lax.dynamic_index_in_dim(hard_blocks, block_index, 0, keepdims=False)
        chosen = text_tiles[listed].astype(jnp.float32)
        image_tiles = image_rows.reshape(TILES_BLK, TILE, E).astype(jnp.float32)
        pair_scores = jnp.einsum('rpe,rkqe->rkpq', image_tiles, chosen)
        pair_low = (temp_scale * jax.nn.sigmoid(temp_scale * pair_scores + shift_bias)).astype(jnp.bfloat16)
        pair_weight = lax.optimization_barrier(pair_low).astype(jnp.float32)
        grad_hard = jnp.einsum('rkpq,rkqe->rpe', pair_weight, chosen).reshape(ROWS, E)
        grad_sel = jnp.einsum('rkpq,rpe->rkqe', pair_weight, image_tiles)
        carried = carried.at[listed.reshape(-1)].add(grad_sel.reshape(TILES_BLK * HARD, TILE, E))
        return (carried, (grad_rows + grad_hard, grad_own))
    initial = jnp.zeros((NTILES, TILE, E), jnp.float32)
    carried, (grad_img_blocks, grad_own_blocks) = lax.scan(one_block, initial, jnp.arange(BLOCKS, dtype=jnp.int32))
    grad_img = grad_img_blocks.reshape(PAIRS, E)
    grad_txt = carried.reshape(PAIRS, E) + grad_own_blocks.reshape(PAIRS, E)
    dots_img = lax.optimization_barrier(jnp.sum(proj_img * grad_img, axis=1))
    dots_txt = lax.optimization_barrier(jnp.sum(proj_txt * grad_txt, axis=1))
    dproj_img = (inv_img[:, None] * grad_img - (dots_img * inv_img * inv_img * inv_img)[:, None] * proj_img).astype(jnp.bfloat16)
    dproj_txt = (inv_txt[:, None] * grad_txt - (dots_txt * inv_txt * inv_txt * inv_txt)[:, None] * proj_txt).astype(jnp.bfloat16)
    head_grad_img = jnp.dot(image_feats.T, dproj_img, preferred_element_type=jnp.float32)
    head_grad_txt = jnp.dot(text_feats.T, dproj_txt, preferred_element_type=jnp.float32)
    return (head_grad_img, head_grad_txt)
```

```python
import jax
import jax.numpy as jnp
from jax import lax
from jax.sharding import Mesh, PartitionSpec as P

EPSILON = 1e-06


DP = ("yh", "z", "x")


def shifted(value, axis, steps):
    count = lax.psum(1, axis)
    pairs = [(source, (source + steps) % count) for source in range(count)]
    return lax.ppermute(value, axis, pairs)


def reduce_rows(local_img, local_txt):
    width = local_img.shape[1]
    sizes = [lax.psum(1, axis) for axis in DP]
    joined = jnp.concatenate([local_img, local_txt], axis=1)
    rows = joined.shape[0] // (sizes[0] * sizes[1] * sizes[2])
    joined = joined.reshape(sizes[0], sizes[1], sizes[2], rows, 2 * width)
    for dim in (2, 1, 0):
        joined = lax.all_to_all(joined, DP[dim], dim, dim, tiled=True).sum(dim, keepdims=True)
    joined = joined.reshape(rows, 2 * width)
    return joined[:, :width], joined[:, width:]


def shards(image_feats, text_feats, image_head, text_head, hard_tiles, logit_scale, logit_bias):
    row_count = image_feats.shape[0]
    width_part = image_head.shape[1]
    per_block = row_count // 128
    model_count = lax.psum(1, "mp")
    model_index = lax.axis_index("mp")
    tiles_share = per_block // model_count
    span_blocks = min(2, (lax.psum(1, DP) - 1) // 2)
    pick_count = hard_tiles.shape[1] // (2 * span_blocks)
    temp_scale = logit_scale[0]
    shift_bias = logit_bias[0]
    image_proj = jnp.dot(image_feats, image_head, preferred_element_type=jnp.float32)
    text_proj = jnp.dot(text_feats, text_head, preferred_element_type=jnp.float32)
    norm_img, norm_txt = lax.psum(
        (jnp.sum(image_proj * image_proj, axis=1), jnp.sum(text_proj * text_proj, axis=1)), "mp"
    )
    inverse_img = lax.rsqrt(norm_img + EPSILON)
    inverse_txt = lax.rsqrt(norm_txt + EPSILON)
    image_unit = (image_proj * inverse_img[:, None]).astype(jnp.bfloat16)
    text_unit = (text_proj * inverse_txt[:, None]).astype(jnp.bfloat16)
    image_tiles = image_unit.reshape(per_block, 128, width_part)
    local_ids = hard_tiles % per_block
    image_mine = lax.all_to_all(image_unit, "mp", split_axis=0, concat_axis=1, tiled=True)
    mine_tiles = image_mine.reshape(tiles_share, 128, image_mine.shape[1])
    text_full = lax.all_gather(text_unit, "mp", axis=1, tiled=True)
    partial_value = jnp.dot(image_unit, text_unit.T, preferred_element_type=jnp.float32)
    scores = lax.psum(partial_value, "mp")
    diagonal_mask = jnp.eye(row_count, dtype=jnp.float32)
    weight = (
        temp_scale * (jax.nn.sigmoid(temp_scale * scores + shift_bias) - diagonal_mask)
    ).astype(jnp.bfloat16)
    grad_img = jnp.dot(weight, text_unit, preferred_element_type=jnp.float32)
    grad_txt = jnp.einsum("pq,pe->qe", weight, image_unit, preferred_element_type=jnp.float32)
    current = shifted(text_full, DP, -span_blocks)
    carried = jnp.zeros_like(text_proj)
    for step_index in range(2 * span_blocks + 1):
        if step_index > 0:
            current = shifted(current, DP, 1)
            carried = shifted(carried, DP, 1)
        offset = span_blocks - step_index
        if offset != 0:
            slot_index = offset + span_blocks if offset < 0 else offset + span_blocks - 1
            picked = local_ids[:, pick_count * slot_index : pick_count * slot_index + pick_count]
            picked_mine = lax.dynamic_slice_in_dim(
                picked, model_index * tiles_share, tiles_share, 0
            )
            wide_tiles = current.reshape(per_block, 128, current.shape[1])
            chosen_wide = jnp.take(wide_tiles, picked_mine, axis=0)
            pair_part = jnp.einsum(
                "rpe,rkqe->rkpq", mine_tiles, chosen_wide, preferred_element_type=jnp.float32
            )
            weight_part = (temp_scale * jax.nn.sigmoid(temp_scale * pair_part + shift_bias)).astype(
                jnp.bfloat16
            )
            pair_weight = lax.all_gather(weight_part, "mp", axis=0, tiled=True)
            text_local = lax.dynamic_slice_in_dim(current, model_index * width_part, width_part, 1)
            chosen = jnp.take(text_local.reshape(per_block, 128, width_part), picked, axis=0)
            into_img = jnp.einsum(
                "rkpq,rkqe->rpe", pair_weight, chosen, preferred_element_type=jnp.float32
            )
            into_sel = jnp.einsum(
                "rkpq,rpe->rkqe", pair_weight, image_tiles, preferred_element_type=jnp.float32
            )
            onehot = (
                picked[:, :, None] == jnp.arange(per_block, dtype=jnp.int32)[None, None, :]
            ).astype(jnp.float32)
            into_txt = jnp.einsum(
                "rkt,rkqe->tqe", onehot, into_sel, precision=lax.Precision.HIGHEST
            )
            into_img, into_txt = (
                into_img.reshape(row_count, width_part),
                into_txt.reshape(row_count, width_part),
            )
            grad_img = grad_img + into_img
            carried = carried + into_txt
    grad_txt = grad_txt + shifted(carried, DP, -span_blocks)
    dots_img, dots_txt = lax.psum(
        (jnp.sum(image_proj * grad_img, axis=1), jnp.sum(text_proj * grad_txt, axis=1)), "mp"
    )
    cube_img = dots_img * inverse_img * inverse_img * inverse_img
    cube_txt = dots_txt * inverse_txt * inverse_txt * inverse_txt
    dproj_img = (inverse_img[:, None] * grad_img - cube_img[:, None] * image_proj).astype(
        jnp.bfloat16
    )
    dproj_txt = (inverse_txt[:, None] * grad_txt - cube_txt[:, None] * text_proj).astype(
        jnp.bfloat16
    )
    local_img = jnp.einsum("nd,ne->de", image_feats, dproj_img, preferred_element_type=jnp.float32)
    local_txt = jnp.einsum("nd,ne->de", text_feats, dproj_txt, preferred_element_type=jnp.float32)
    head_grad_img, head_grad_txt = reduce_rows(local_img, local_txt)
    return (head_grad_img, head_grad_txt)


def solution(mesh):
    dp_size = mesh.shape["dp"]
    x_size = 4 if dp_size % 4 == 0 else 1
    y_size = 2 if dp_size % (2 * x_size) == 0 and dp_size > 2 * x_size else 1
    z_size = dp_size // (x_size * y_size)
    split_mesh = Mesh(
        mesh.devices.reshape(y_size, z_size, x_size, mesh.shape["mp"]), DP + ("mp",)
    )
    placed = (P(DP, None), P(DP, None), P(None, "mp"), P(None, "mp"), P(DP, None), P(), P())
    return jax.shard_map(
        shards,
        mesh=split_mesh,
        in_specs=placed,
        out_specs=(P(DP, "mp"), P(DP, "mp")),
        check_vma=False,
    )
```

```python
import jax
import jax.numpy as jnp
from jax import lax
from jax.sharding import Mesh, PartitionSpec as P

EPSILON = 1e-06
DP = ("yh", "z", "x")
ALL = DP + ("mp",)


def shifted(value, axis, steps):
    count = lax.psum(1, axis)
    pairs = [(source, (source + steps) % count) for source in range(count)]
    return lax.ppermute(value, axis, pairs)


def reduce_rows(local_img, local_txt):
    width = local_img.shape[1]
    sizes = [lax.psum(1, axis) for axis in DP]
    joined = jnp.concatenate([local_img, local_txt], axis=1)
    rows = joined.shape[0] // (sizes[0] * sizes[1] * sizes[2])
    joined = joined.reshape(sizes[0], sizes[1], sizes[2], rows, 2 * width)
    for dim in (2, 1, 0):
        joined = lax.all_to_all(joined, DP[dim], dim, dim, tiled=True).sum(dim, keepdims=True)
    joined = joined.reshape(rows, 2 * width)
    return joined[:, :width], joined[:, width:]


def embed(features, head):
    projected = jnp.dot(features, head, preferred_element_type=jnp.float32)
    inverse = lax.rsqrt(jnp.sum(projected * projected, axis=1) + EPSILON)
    unit = (projected * inverse[:, None]).astype(jnp.bfloat16)
    return projected, inverse, unit


def shards(image_feats, text_feats, image_head, text_head, hard_tiles, logit_scale, logit_bias):
    row_count = image_feats.shape[0]
    width_part = image_head.shape[1]
    per_block = row_count // 128
    model_count = lax.psum(1, "mp")
    model_index = lax.axis_index("mp")
    block_count = lax.psum(1, DP)
    share = row_count // model_count
    offsets = (-2, -1, 1, 2)
    slot_of_model = (0, 2, 1, 3)
    model_of_slot = tuple(slot_of_model.index(s) for s in range(4))
    pick_count = hard_tiles.shape[1] // len(offsets)
    temp_scale = logit_scale[0]
    shift_bias = logit_bias[0]

    head_img, head_txt = lax.all_gather((image_head, text_head), "mp", axis=1, tiled=True)
    image_proj, inverse_img, image_unit = embed(image_feats, head_img)
    text_proj, inverse_txt, text_unit = embed(text_feats, head_txt)

    pairs = []
    for block in range(block_count):
        for model in range(model_count):
            source = ((block + offsets[slot_of_model[model]]) % block_count) * model_count + model
            pairs.append((source, block * model_count + model))
    text_near = lax.ppermute(text_unit, ALL, pairs)

    local_ids = hard_tiles % per_block
    my_slot = jnp.array(slot_of_model, jnp.int32)[model_index]
    my_picks = lax.dynamic_slice_in_dim(local_ids, my_slot * pick_count, pick_count, 1)
    image_tiles_full = image_unit.reshape(per_block, 128, image_unit.shape[1])
    near_tiles = text_near.reshape(per_block, 128, text_near.shape[1])
    chosen_full = jnp.take(near_tiles, my_picks, axis=0)
    pair_scores = jnp.einsum(
        "rpe,rkqe->rkpq", image_tiles_full, chosen_full, preferred_element_type=jnp.float32
    )
    hard_weight = (temp_scale * jax.nn.sigmoid(temp_scale * pair_scores + shift_bias)).astype(
        jnp.bfloat16
    )

    image_mine = lax.dynamic_slice_in_dim(image_unit, model_index * share, share, 0)
    own_scores = jnp.dot(image_mine, text_unit.T, preferred_element_type=jnp.float32)
    diagonal_mask = (
        jnp.arange(row_count, dtype=jnp.int32)[None, :]
        == (jnp.arange(share, dtype=jnp.int32) + model_index * share)[:, None]
    ).astype(jnp.float32)
    own_weight = (
        temp_scale * (jax.nn.sigmoid(temp_scale * own_scores + shift_bias) - diagonal_mask)
    ).astype(jnp.bfloat16)

    own_size = own_weight.size
    packed = jnp.concatenate([own_weight.reshape(-1), hard_weight.reshape(-1)])
    gathered = lax.all_gather(packed, "mp", axis=0, tiled=False)
    weight = gathered[:, :own_size].reshape(row_count, row_count)
    hard_all = gathered[:, own_size:].reshape((model_count,) + hard_weight.shape)

    text_split = text_near.reshape(row_count, model_count, width_part)
    text_split = lax.all_to_all(text_split, "mp", 1, 1, tiled=True)

    e_start = model_index * width_part
    text_local = lax.dynamic_slice_in_dim(text_unit, e_start, width_part, 1)
    image_local = lax.dynamic_slice_in_dim(image_unit, e_start, width_part, 1)
    proj_img = lax.dynamic_slice_in_dim(image_proj, e_start, width_part, 1)
    proj_txt = lax.dynamic_slice_in_dim(text_proj, e_start, width_part, 1)
    image_tiles = image_local.reshape(per_block, 128, width_part)

    grad_img = jnp.dot(weight, text_local, preferred_element_type=jnp.float32)
    grad_txt = jnp.einsum("pq,pe->qe", weight, image_local, preferred_element_type=jnp.float32)
    for slot, offset in enumerate(offsets):
        source_model = model_of_slot[slot]
        pair_weight = hard_all[source_model]
        picked = local_ids[:, pick_count * slot : pick_count * slot + pick_count]
        near_local = text_split[:, source_model, :].reshape(per_block, 128, width_part)
        chosen = jnp.take(near_local, picked, axis=0)
        into_img = jnp.einsum(
            "rkpq,rkqe->rpe", pair_weight, chosen, preferred_element_type=jnp.float32
        )
        into_sel = jnp.einsum(
            "rkpq,rpe->rkqe", pair_weight, image_tiles, preferred_element_type=jnp.float32
        )
        onehot = (
            picked[:, :, None] == jnp.arange(per_block, dtype=jnp.int32)[None, None, :]
        ).astype(jnp.float32)
        into_txt = jnp.einsum("rkt,rkqe->tqe", onehot, into_sel, precision=lax.Precision.HIGHEST)
        grad_img = grad_img + into_img.reshape(row_count, width_part)
        grad_txt = grad_txt + shifted(into_txt.reshape(row_count, width_part), DP, offset)

    dots_img, dots_txt = lax.psum(
        (jnp.sum(proj_img * grad_img, axis=1), jnp.sum(proj_txt * grad_txt, axis=1)), "mp"
    )
    cube_img = dots_img * inverse_img * inverse_img * inverse_img
    cube_txt = dots_txt * inverse_txt * inverse_txt * inverse_txt
    dproj_img = (inverse_img[:, None] * grad_img - cube_img[:, None] * proj_img).astype(
        jnp.bfloat16
    )
    dproj_txt = (inverse_txt[:, None] * grad_txt - cube_txt[:, None] * proj_txt).astype(
        jnp.bfloat16
    )
    local_img = jnp.einsum("nd,ne->de", image_feats, dproj_img, preferred_element_type=jnp.float32)
    local_txt = jnp.einsum("nd,ne->de", text_feats, dproj_txt, preferred_element_type=jnp.float32)
    return reduce_rows(local_img, local_txt)


def solution(mesh):
    dp_size = mesh.shape["dp"]
    x_size = 4 if dp_size % 4 == 0 else 1
    y_size = 2 if dp_size % (2 * x_size) == 0 and dp_size > 2 * x_size else 1
    z_size = dp_size // (x_size * y_size)
    split_mesh = Mesh(
        mesh.devices.reshape(y_size, z_size, x_size, mesh.shape["mp"]), DP + ("mp",)
    )
    placed = (P(DP, None), P(DP, None), P(None, "mp"), P(None, "mp"), P(DP, None), P(), P())
    return jax.shard_map(
        shards,
        mesh=split_mesh,
        in_specs=placed,
        out_specs=(P(DP, "mp"), P(DP, "mp")),
        check_vma=False,
    )
```

```python
import jax
import jax.numpy as jnp
from jax import lax
from jax.sharding import Mesh, PartitionSpec as P

EPSILON = 1e-06
DP = ("yh", "z", "x")
ALL = DP + ("mp",)


def shifted(value, axis, steps):
    count = lax.psum(1, axis)
    pairs = [(source, (source + steps) % count) for source in range(count)]
    return lax.ppermute(value, axis, pairs)


def reduce_rows(local):
    width = local.shape[1]
    sizes = [lax.psum(1, axis) for axis in DP]
    rows = local.shape[0] // (sizes[0] * sizes[1] * sizes[2])
    joined = local.reshape(sizes[0], sizes[1], sizes[2], rows, width)
    for dim in (2, 1, 0):
        joined = lax.all_to_all(joined, DP[dim], dim, dim, tiled=True).sum(dim, keepdims=True)
    return joined.reshape(rows, width)


def embed(features, head):
    projected = jnp.dot(features, head, preferred_element_type=jnp.float32)
    inverse = lax.rsqrt(jnp.sum(projected * projected, axis=1) + EPSILON)
    unit = (projected * inverse[:, None]).astype(jnp.bfloat16)
    return projected, inverse, unit


def shards(image_feats, text_feats, image_head, text_head, hard_tiles, logit_scale, logit_bias):
    row_count = image_feats.shape[0]
    width_part = image_head.shape[1]
    per_block = row_count // 128
    model_count = lax.psum(1, "mp")
    model_index = lax.axis_index("mp")
    block_count = lax.psum(1, DP)
    share = row_count // model_count
    offsets = (-2, -1, 1, 2)
    slot_of_model = (0, 2, 1, 3)
    model_of_slot = tuple(slot_of_model.index(s) for s in range(4))
    pick_count = hard_tiles.shape[1] // len(offsets)
    temp_scale = logit_scale[0]
    shift_bias = logit_bias[0]

    heads = lax.all_gather(jnp.stack([image_head, text_head]), "mp", axis=0, tiled=False)
    heads = jnp.transpose(heads, (1, 2, 0, 3)).reshape(2, image_head.shape[0], -1)
    head_img, head_txt = heads[0], heads[1]
    image_proj, inverse_img, image_unit = embed(image_feats, head_img)
    text_proj, inverse_txt, text_unit = embed(text_feats, head_txt)

    pairs = []
    for block in range(block_count):
        for model in range(model_count):
            source = ((block + offsets[slot_of_model[model]]) % block_count) * model_count + model
            pairs.append((source, block * model_count + model))
    text_near = lax.ppermute(text_unit, ALL, pairs)

    local_ids = hard_tiles % per_block
    my_slot = jnp.array(slot_of_model, jnp.int32)[model_index]
    my_picks = lax.dynamic_slice_in_dim(local_ids, my_slot * pick_count, pick_count, 1)
    image_tiles_full = image_unit.reshape(per_block, 128, image_unit.shape[1])
    near_tiles = text_near.reshape(per_block, 128, text_near.shape[1])
    chosen_full = jnp.take(near_tiles, my_picks, axis=0)
    pair_scores = jnp.einsum(
        "rpe,rkqe->rkpq", image_tiles_full, chosen_full, preferred_element_type=jnp.float32
    )
    hard_weight = (temp_scale * jax.nn.sigmoid(temp_scale * pair_scores + shift_bias)).astype(
        jnp.bfloat16
    )

    own_scores = jnp.dot(image_unit, text_unit.T, preferred_element_type=jnp.float32)
    diagonal_mask = jnp.eye(row_count, dtype=jnp.float32)
    weight = (
        temp_scale * (jax.nn.sigmoid(temp_scale * own_scores + shift_bias) - diagonal_mask)
    ).astype(jnp.bfloat16)

    hard_all = lax.all_gather(hard_weight, "mp", axis=0, tiled=False)

    text_split = text_near.reshape(row_count, model_count, width_part)
    text_split = lax.all_to_all(text_split, "mp", 1, 1, tiled=True)

    e_start = model_index * width_part
    text_local = lax.dynamic_slice_in_dim(text_unit, e_start, width_part, 1)
    image_local = lax.dynamic_slice_in_dim(image_unit, e_start, width_part, 1)
    proj_img = lax.dynamic_slice_in_dim(image_proj, e_start, width_part, 1)
    proj_txt = lax.dynamic_slice_in_dim(text_proj, e_start, width_part, 1)
    image_tiles = image_local.reshape(per_block, 128, width_part)

    grad_img = jnp.dot(weight, text_local, preferred_element_type=jnp.float32)
    grad_txt = jnp.einsum("pq,pe->qe", weight, image_local, preferred_element_type=jnp.float32)
    for slot, offset in enumerate(offsets):
        source_model = model_of_slot[slot]
        pair_weight = hard_all[source_model]
        picked = local_ids[:, pick_count * slot : pick_count * slot + pick_count]
        near_local = text_split[:, source_model, :].reshape(per_block, 128, width_part)
        chosen = jnp.take(near_local, picked, axis=0)
        into_img = jnp.einsum(
            "rkpq,rkqe->rpe", pair_weight, chosen, preferred_element_type=jnp.float32
        )
        into_sel = jnp.einsum(
            "rkpq,rpe->rkqe", pair_weight, image_tiles, preferred_element_type=jnp.float32
        )
        onehot = (
            picked[:, :, None] == jnp.arange(per_block, dtype=jnp.int32)[None, None, :]
        ).astype(jnp.float32)
        into_txt = jnp.einsum("rkt,rkqe->tqe", onehot, into_sel, precision=lax.Precision.HIGHEST)
        grad_img = grad_img + into_img.reshape(row_count, width_part)
        grad_txt = grad_txt + shifted(into_txt.reshape(row_count, width_part), DP, offset)

    img_part = tail(image_feats, proj_img, inverse_img, grad_img)
    txt_part = tail(text_feats, proj_txt, inverse_txt, grad_txt)
    return img_part, txt_part


def tail(features, projected, inverse, grad):
    dots = lax.psum(jnp.sum(projected * grad, axis=1), "mp")
    cube = dots * inverse * inverse * inverse
    dproj = (inverse[:, None] * grad - cube[:, None] * projected).astype(jnp.bfloat16)
    local = jnp.einsum("nd,ne->de", features, dproj, preferred_element_type=jnp.float32)
    return reduce_rows(local)


def solution(mesh):
    dp_size = mesh.shape["dp"]
    x_size = 4 if dp_size % 4 == 0 else 1
    y_size = 2 if dp_size % (2 * x_size) == 0 and dp_size > 2 * x_size else 1
    z_size = dp_size // (x_size * y_size)
    split_mesh = Mesh(
        mesh.devices.reshape(y_size, z_size, x_size, mesh.shape["mp"]), DP + ("mp",)
    )
    placed = (P(DP, None), P(DP, None), P(None, "mp"), P(None, "mp"), P(DP, None), P(), P())
    return jax.shard_map(
        shards,
        mesh=split_mesh,
        in_specs=placed,
        out_specs=(P(DP, "mp"), P(DP, "mp")),
        check_vma=False,
    )
```

```python
import jax
import jax.numpy as jnp
from jax import lax
from jax.sharding import Mesh, PartitionSpec as P

EPSILON = 1e-06
DP = ("yh", "z", "x")
ALL = DP + ("mp",)


def shifted(value, axis, steps):
    count = lax.psum(1, axis)
    pairs = [(source, (source + steps) % count) for source in range(count)]
    return lax.ppermute(value, axis, pairs)


def reduce_rows(local):
    width = local.shape[1]
    sizes = [lax.psum(1, axis) for axis in DP]
    rows = local.shape[0] // (sizes[0] * sizes[1] * sizes[2])
    joined = local.reshape(sizes[0], sizes[1], sizes[2], rows, width)
    for dim in (2, 1, 0):
        joined = lax.all_to_all(joined, DP[dim], dim, dim, tiled=True).sum(dim, keepdims=True)
    return joined.reshape(rows, width)


def embed(features, head):
    projected = jnp.dot(features, head, preferred_element_type=jnp.float32)
    inverse = lax.rsqrt(jnp.sum(projected * projected, axis=1) + EPSILON)
    unit = (projected * inverse[:, None]).astype(jnp.bfloat16)
    return projected, inverse, unit


def shards(image_feats, text_feats, image_head, text_head, hard_tiles, logit_scale, logit_bias):
    row_count = image_feats.shape[0]
    width_part = image_head.shape[1]
    per_block = row_count // 128
    model_count = lax.psum(1, "mp")
    model_index = lax.axis_index("mp")
    block_count = lax.psum(1, DP)
    share = row_count // model_count
    offsets = (-2, -1, 1, 2)
    slot_of_model = (0, 2, 1, 3)
    model_of_slot = tuple(slot_of_model.index(s) for s in range(4))
    pick_count = hard_tiles.shape[1] // len(offsets)
    temp_scale = logit_scale[0]
    shift_bias = logit_bias[0]

    heads = lax.all_gather(jnp.stack([image_head, text_head]), "mp", axis=0, tiled=False)
    heads = jnp.transpose(heads, (1, 2, 0, 3)).reshape(2, image_head.shape[0], -1)
    head_img, head_txt = heads[0], heads[1]
    image_proj, inverse_img, image_unit = embed(image_feats, head_img)
    text_proj, inverse_txt, text_unit = embed(text_feats, head_txt)

    pairs = []
    for block in range(block_count):
        for model in range(model_count):
            source = ((block + offsets[slot_of_model[model]]) % block_count) * model_count + model
            pairs.append((source, block * model_count + model))
    text_near = lax.ppermute(text_unit, ALL, pairs)

    local_ids = hard_tiles % per_block
    my_slot = jnp.array(slot_of_model, jnp.int32)[model_index]
    my_picks = lax.dynamic_slice_in_dim(local_ids, my_slot * pick_count, pick_count, 1)
    image_tiles_full = image_unit.reshape(per_block, 128, image_unit.shape[1])
    near_tiles = text_near.reshape(per_block, 128, text_near.shape[1])
    chosen_full = jnp.take(near_tiles, my_picks, axis=0)
    pair_scores = jnp.einsum(
        "rpe,rkqe->rkpq", image_tiles_full, chosen_full, preferred_element_type=jnp.float32
    )
    hard_weight = (temp_scale * jax.nn.sigmoid(temp_scale * pair_scores + shift_bias)).astype(
        jnp.bfloat16
    )

    own_scores = jnp.dot(image_unit, text_unit.T, preferred_element_type=jnp.float32)
    diagonal_mask = jnp.eye(row_count, dtype=jnp.float32)
    weight = (
        temp_scale * (jax.nn.sigmoid(temp_scale * own_scores + shift_bias) - diagonal_mask)
    ).astype(jnp.bfloat16)

    hard_all = lax.all_gather(hard_weight, "mp", axis=0, tiled=False)

    text_split = text_near.reshape(row_count, model_count, width_part)
    text_split = lax.all_to_all(text_split, "mp", 1, 1, tiled=True)

    e_start = model_index * width_part
    text_local = lax.dynamic_slice_in_dim(text_unit, e_start, width_part, 1)
    image_local = lax.dynamic_slice_in_dim(image_unit, e_start, width_part, 1)
    proj_img = lax.dynamic_slice_in_dim(image_proj, e_start, width_part, 1)
    proj_txt = lax.dynamic_slice_in_dim(text_proj, e_start, width_part, 1)
    image_tiles = image_local.reshape(per_block, 128, width_part)

    grad_img = jnp.dot(weight, text_local, preferred_element_type=jnp.float32)
    grad_txt = jnp.einsum("pq,pe->qe", weight, image_local, preferred_element_type=jnp.float32)
    for slot, offset in enumerate(offsets):
        source_model = model_of_slot[slot]
        pair_weight = hard_all[source_model]
        picked = local_ids[:, pick_count * slot : pick_count * slot + pick_count]
        near_local = text_split[:, source_model, :].reshape(per_block, 128, width_part)
        chosen = jnp.take(near_local, picked, axis=0)
        into_img = jnp.einsum(
            "rkpq,rkqe->rpe", pair_weight, chosen, preferred_element_type=jnp.float32
        )
        into_sel = jnp.einsum(
            "rkpq,rpe->rkqe", pair_weight, image_tiles, preferred_element_type=jnp.float32
        )
        onehot = (
            picked[:, :, None] == jnp.arange(per_block, dtype=jnp.int32)[None, None, :]
        ).astype(jnp.float32)
        into_txt = jnp.einsum("rkt,rkqe->tqe", onehot, into_sel, precision=lax.Precision.HIGHEST)
        grad_img = grad_img + into_img.reshape(row_count, width_part)
        grad_txt = grad_txt + shifted(into_txt.reshape(row_count, width_part), DP, offset)

    dots_img, dots_txt = lax.psum(
        (jnp.sum(proj_img * grad_img, axis=1), jnp.sum(proj_txt * grad_txt, axis=1)), "mp"
    )
    local_img = head_part(image_feats, proj_img, inverse_img, grad_img, dots_img)
    local_txt = head_part(text_feats, proj_txt, inverse_txt, grad_txt, dots_txt)
    joined = reduce_rows(jnp.concatenate([local_img, local_txt], axis=1))
    return joined[:, :width_part], joined[:, width_part:]


def head_part(features, projected, inverse, grad, dots):
    cube = dots * inverse * inverse * inverse
    dproj = (inverse[:, None] * grad - cube[:, None] * projected).astype(jnp.bfloat16)
    return jnp.einsum("nd,ne->de", features, dproj, preferred_element_type=jnp.float32)


def solution(mesh):
    dp_size = mesh.shape["dp"]
    x_size = 4 if dp_size % 4 == 0 else 1
    y_size = 2 if dp_size % (2 * x_size) == 0 and dp_size > 2 * x_size else 1
    z_size = dp_size // (x_size * y_size)
    split_mesh = Mesh(
        mesh.devices.reshape(y_size, z_size, x_size, mesh.shape["mp"]), DP + ("mp",)
    )
    placed = (P(DP, None), P(DP, None), P(None, "mp"), P(None, "mp"), P(DP, None), P(), P())
    return jax.shard_map(
        shards,
        mesh=split_mesh,
        in_specs=placed,
        out_specs=(P(DP, "mp"), P(DP, "mp")),
        check_vma=False,
    )
```

```python
import jax
import jax.numpy as jnp
from jax import lax
from jax.sharding import Mesh, PartitionSpec as P

EPSILON = 1e-06
DP = ("yh", "z", "x")
ALL = DP + ("mp",)


def shifted(value, axis, steps):
    count = lax.psum(1, axis)
    pairs = [(source, (source + steps) % count) for source in range(count)]
    return lax.ppermute(value, axis, pairs)


def reduce_rows(local):
    width = local.shape[1]
    sizes = [lax.psum(1, axis) for axis in DP]
    rows = local.shape[0] // (sizes[0] * sizes[1] * sizes[2])
    joined = local.reshape(sizes[0], sizes[1], sizes[2], rows, width)
    for dim in (2, 1, 0):
        joined = lax.all_to_all(joined, DP[dim], dim, dim, tiled=True).sum(dim, keepdims=True)
    return joined.reshape(rows, width)


def embed(features, head):
    projected = jnp.dot(features, head, preferred_element_type=jnp.float32)
    inverse = lax.rsqrt(jnp.sum(projected * projected, axis=1) + EPSILON)
    unit = (projected * inverse[:, None]).astype(jnp.bfloat16)
    return projected, inverse, unit


def shards(image_feats, text_feats, image_head, text_head, hard_tiles, logit_scale, logit_bias):
    row_count = image_feats.shape[0]
    width_part = image_head.shape[1]
    per_block = row_count // 128
    model_count = lax.psum(1, "mp")
    model_index = lax.axis_index("mp")
    block_count = lax.psum(1, DP)
    share = row_count // model_count
    offsets = (-2, -1, 1, 2)
    slot_of_model = (0, 2, 1, 3)
    model_of_slot = tuple(slot_of_model.index(s) for s in range(4))
    pick_count = hard_tiles.shape[1] // len(offsets)
    temp_scale = logit_scale[0]
    shift_bias = logit_bias[0]

    pairs = []
    for block in range(block_count):
        for model in range(model_count):
            source = ((block + offsets[slot_of_model[model]]) % block_count) * model_count + model
            pairs.append((source, block * model_count + model))
    feats_near = lax.ppermute(text_feats, ALL, pairs)

    heads = lax.all_gather(jnp.stack([image_head, text_head]), "mp", axis=0, tiled=False)
    heads = jnp.transpose(heads, (1, 2, 0, 3)).reshape(2, image_head.shape[0], -1)
    head_img, head_txt = heads[0], heads[1]
    image_proj, inverse_img, image_unit = embed(image_feats, head_img)
    text_proj, inverse_txt, text_unit = embed(text_feats, head_txt)
    text_near = embed(feats_near, head_txt)[2]

    local_ids = hard_tiles % per_block
    my_slot = jnp.array(slot_of_model, jnp.int32)[model_index]
    my_picks = lax.dynamic_slice_in_dim(local_ids, my_slot * pick_count, pick_count, 1)
    image_tiles_full = image_unit.reshape(per_block, 128, image_unit.shape[1])
    near_tiles = text_near.reshape(per_block, 128, text_near.shape[1])
    chosen_full = jnp.take(near_tiles, my_picks, axis=0)
    pair_scores = jnp.einsum(
        "rpe,rkqe->rkpq", image_tiles_full, chosen_full, preferred_element_type=jnp.float32
    )
    hard_weight = (temp_scale * jax.nn.sigmoid(temp_scale * pair_scores + shift_bias)).astype(
        jnp.bfloat16
    )

    own_scores = jnp.dot(image_unit, text_unit.T, preferred_element_type=jnp.float32)
    diagonal_mask = jnp.eye(row_count, dtype=jnp.float32)
    weight = (
        temp_scale * (jax.nn.sigmoid(temp_scale * own_scores + shift_bias) - diagonal_mask)
    ).astype(jnp.bfloat16)

    hard_all = lax.all_gather(hard_weight, "mp", axis=0, tiled=False)

    text_split = text_near.reshape(row_count, model_count, width_part)
    text_split = lax.all_to_all(text_split, "mp", 1, 1, tiled=True)

    e_start = model_index * width_part
    text_local = lax.dynamic_slice_in_dim(text_unit, e_start, width_part, 1)
    image_local = lax.dynamic_slice_in_dim(image_unit, e_start, width_part, 1)
    proj_img = lax.dynamic_slice_in_dim(image_proj, e_start, width_part, 1)
    proj_txt = lax.dynamic_slice_in_dim(text_proj, e_start, width_part, 1)
    image_tiles = image_local.reshape(per_block, 128, width_part)

    grad_img = jnp.dot(weight, text_local, preferred_element_type=jnp.float32)
    grad_txt = jnp.einsum("pq,pe->qe", weight, image_local, preferred_element_type=jnp.float32)
    returned = []
    for slot, offset in enumerate(offsets):
        source_model = model_of_slot[slot]
        pair_weight = hard_all[source_model]
        picked = local_ids[:, pick_count * slot : pick_count * slot + pick_count]
        near_local = text_split[:, source_model, :].reshape(per_block, 128, width_part)
        chosen = jnp.take(near_local, picked, axis=0)
        into_img = jnp.einsum(
            "rkpq,rkqe->rpe", pair_weight, chosen, preferred_element_type=jnp.float32
        )
        into_sel = jnp.einsum(
            "rkpq,rpe->rkqe", pair_weight, image_tiles, preferred_element_type=jnp.float32
        )
        onehot = (
            picked[:, :, None] == jnp.arange(per_block, dtype=jnp.int32)[None, None, :]
        ).astype(jnp.float32)
        into_txt = jnp.einsum("rkt,rkqe->tqe", onehot, into_sel, precision=lax.Precision.HIGHEST)
        grad_img = grad_img + into_img.reshape(row_count, width_part)
        returned.append(shifted(into_txt.reshape(row_count, width_part), DP, offset))

    dots_img = lax.psum(jnp.sum(proj_img * grad_img, axis=1), "mp")
    local_img = head_part(image_feats, proj_img, inverse_img, grad_img, dots_img)
    out_img = reduce_rows(local_img)
    for part in returned:
        grad_txt = grad_txt + part
    dots_part = jnp.sum(proj_txt * grad_txt, axis=1)
    dots_img, dots_part = lax.optimization_barrier((dots_img, dots_part))
    dots_txt = lax.psum(dots_part, "mp")
    local_txt = head_part(text_feats, proj_txt, inverse_txt, grad_txt, dots_txt)
    return out_img, reduce_rows(local_txt)


def head_part(features, projected, inverse, grad, dots):
    cube = dots * inverse * inverse * inverse
    dproj = (inverse[:, None] * grad - cube[:, None] * projected).astype(jnp.bfloat16)
    return jnp.einsum("nd,ne->de", features, dproj, preferred_element_type=jnp.float32)


def solution(mesh):
    dp_size = mesh.shape["dp"]
    x_size = 4 if dp_size % 4 == 0 else 1
    y_size = 2 if dp_size % (2 * x_size) == 0 and dp_size > 2 * x_size else 1
    z_size = dp_size // (x_size * y_size)
    split_mesh = Mesh(
        mesh.devices.reshape(y_size, z_size, x_size, mesh.shape["mp"]), DP + ("mp",)
    )
    placed = (P(DP, None), P(DP, None), P(None, "mp"), P(None, "mp"), P(DP, None), P(), P())
    return jax.shard_map(
        shards,
        mesh=split_mesh,
        in_specs=placed,
        out_specs=(P(DP, "mp"), P(DP, "mp")),
        check_vma=False,
    )
```

```python
import jax
import jax.numpy as jnp
from jax import lax
from jax.sharding import Mesh, PartitionSpec as P

EPSILON = 1e-06
DP = ("yh", "z", "x")
ALL = DP + ("mp",)


def shifted(value, axis, steps):
    count = lax.psum(1, axis)
    pairs = [(source, (source + steps) % count) for source in range(count)]
    return lax.ppermute(value, axis, pairs)


def reduce_rows(local):
    width = local.shape[1]
    sizes = [lax.psum(1, axis) for axis in DP]
    rows = local.shape[0] // (sizes[0] * sizes[1] * sizes[2])
    joined = local.reshape(sizes[0], sizes[1], sizes[2], rows, width)
    for dim in (2, 1, 0):
        joined = lax.all_to_all(joined, DP[dim], dim, dim, tiled=True).sum(dim, keepdims=True)
    return joined.reshape(rows, width)


def embed(features, head):
    projected = jnp.dot(features, head, preferred_element_type=jnp.float32)
    inverse = lax.rsqrt(jnp.sum(projected * projected, axis=1) + EPSILON)
    unit = (projected * inverse[:, None]).astype(jnp.bfloat16)
    return projected, inverse, unit


def shards(image_feats, text_feats, image_head, text_head, hard_tiles, logit_scale, logit_bias):
    row_count = image_feats.shape[0]
    width_part = image_head.shape[1]
    per_block = row_count // 128
    model_count = lax.psum(1, "mp")
    model_index = lax.axis_index("mp")
    block_count = lax.psum(1, DP)
    share = row_count // model_count
    offsets = (-2, -1, 1, 2)
    slot_of_model = (0, 2, 1, 3)
    model_of_slot = tuple(slot_of_model.index(s) for s in range(4))
    pick_count = hard_tiles.shape[1] // len(offsets)
    temp_scale = logit_scale[0]
    shift_bias = logit_bias[0]

    pairs = []
    for block in range(block_count):
        for model in range(model_count):
            source = ((block + offsets[slot_of_model[model]]) % block_count) * model_count + model
            pairs.append((source, block * model_count + model))
    feats_near = lax.ppermute(text_feats, ALL, pairs)

    both = jnp.stack([image_head, text_head])
    by_shift = [both] + [
        lax.ppermute(both, "mp", [(a, (a + s) % model_count) for a in range(model_count)])
        for s in range(1, model_count)
    ]
    order = (model_index - jnp.arange(model_count, dtype=jnp.int32)) % model_count
    heads = jnp.take(jnp.stack(by_shift), order, axis=0)
    heads = jnp.transpose(heads, (1, 2, 0, 3)).reshape(2, image_head.shape[0], -1)
    head_img, head_txt = heads[0], heads[1]
    image_proj, inverse_img, image_unit = embed(image_feats, head_img)
    text_proj, inverse_txt, text_unit = embed(text_feats, head_txt)
    text_near = embed(feats_near, head_txt)[2]

    local_ids = hard_tiles % per_block
    my_slot = jnp.array(slot_of_model, jnp.int32)[model_index]
    my_picks = lax.dynamic_slice_in_dim(local_ids, my_slot * pick_count, pick_count, 1)
    image_tiles_full = image_unit.reshape(per_block, 128, image_unit.shape[1])
    near_tiles = text_near.reshape(per_block, 128, text_near.shape[1])
    chosen_full = jnp.take(near_tiles, my_picks, axis=0)
    pair_scores = jnp.einsum(
        "rpe,rkqe->rkpq", image_tiles_full, chosen_full, preferred_element_type=jnp.float32
    )
    hard_weight = (temp_scale * jax.nn.sigmoid(temp_scale * pair_scores + shift_bias)).astype(
        jnp.bfloat16
    )

    own_scores = jnp.dot(image_unit, text_unit.T, preferred_element_type=jnp.float32)
    diagonal_mask = jnp.eye(row_count, dtype=jnp.float32)
    weight = (
        temp_scale * (jax.nn.sigmoid(temp_scale * own_scores + shift_bias) - diagonal_mask)
    ).astype(jnp.bfloat16)

    hard_all = lax.all_gather(hard_weight, "mp", axis=0, tiled=False)

    text_split = text_near.reshape(row_count, model_count, width_part)
    text_split = lax.all_to_all(text_split, "mp", 1, 1, tiled=True)

    e_start = model_index * width_part
    text_local = lax.dynamic_slice_in_dim(text_unit, e_start, width_part, 1)
    image_local = lax.dynamic_slice_in_dim(image_unit, e_start, width_part, 1)
    proj_img = lax.dynamic_slice_in_dim(image_proj, e_start, width_part, 1)
    proj_txt = lax.dynamic_slice_in_dim(text_proj, e_start, width_part, 1)
    image_tiles = image_local.reshape(per_block, 128, width_part)

    grad_img = jnp.dot(weight, text_local, preferred_element_type=jnp.float32)
    grad_txt = jnp.einsum("pq,pe->qe", weight, image_local, preferred_element_type=jnp.float32)
    returned = []
    for slot, offset in enumerate(offsets):
        source_model = model_of_slot[slot]
        pair_weight = hard_all[source_model]
        picked = local_ids[:, pick_count * slot : pick_count * slot + pick_count]
        near_local = text_split[:, source_model, :].reshape(per_block, 128, width_part)
        chosen = jnp.take(near_local, picked, axis=0)
        into_img = jnp.einsum(
            "rkpq,rkqe->rpe", pair_weight, chosen, preferred_element_type=jnp.float32
        )
        into_sel = jnp.einsum(
            "rkpq,rpe->rkqe", pair_weight, image_tiles, preferred_element_type=jnp.float32
        )
        onehot = (
            picked[:, :, None] == jnp.arange(per_block, dtype=jnp.int32)[None, None, :]
        ).astype(jnp.float32)
        into_txt = jnp.einsum("rkt,rkqe->tqe", onehot, into_sel, precision=lax.Precision.HIGHEST)
        grad_img = grad_img + into_img.reshape(row_count, width_part)
        returned.append(shifted(into_txt.reshape(row_count, width_part), DP, offset))

    dots_img = lax.psum(jnp.sum(proj_img * grad_img, axis=1), "mp")
    local_img = head_part(image_feats, proj_img, inverse_img, grad_img, dots_img)
    out_img = reduce_rows(local_img)
    for part in returned:
        grad_txt = grad_txt + part
    dots_part = jnp.sum(proj_txt * grad_txt, axis=1)
    dots_img, dots_part = lax.optimization_barrier((dots_img, dots_part))
    dots_txt = lax.psum(dots_part, "mp")
    local_txt = head_part(text_feats, proj_txt, inverse_txt, grad_txt, dots_txt)
    return out_img, reduce_rows(local_txt)


def head_part(features, projected, inverse, grad, dots):
    cube = dots * inverse * inverse * inverse
    dproj = (inverse[:, None] * grad - cube[:, None] * projected).astype(jnp.bfloat16)
    return jnp.einsum("nd,ne->de", features, dproj, preferred_element_type=jnp.float32)


def solution(mesh):
    dp_size = mesh.shape["dp"]
    x_size = 4 if dp_size % 4 == 0 else 1
    y_size = 2 if dp_size % (2 * x_size) == 0 and dp_size > 2 * x_size else 1
    z_size = dp_size // (x_size * y_size)
    split_mesh = Mesh(
        mesh.devices.reshape(y_size, z_size, x_size, mesh.shape["mp"]), DP + ("mp",)
    )
    placed = (P(DP, None), P(DP, None), P(None, "mp"), P(None, "mp"), P(DP, None), P(), P())
    return jax.shard_map(
        shards,
        mesh=split_mesh,
        in_specs=placed,
        out_specs=(P(DP, "mp"), P(DP, "mp")),
        check_vma=False,
    )
```

```python
import jax
import jax.numpy as jnp
from jax import lax
from jax.sharding import Mesh, PartitionSpec as P

EPSILON = 1e-06
DP = ("yh", "z", "x")
ALL = DP + ("mp",)


def shifted(value, axis, steps):
    count = lax.psum(1, axis)
    pairs = [(source, (source + steps) % count) for source in range(count)]
    return lax.ppermute(value, axis, pairs)


def reduce_rows(local):
    width = local.shape[1]
    sizes = [lax.psum(1, axis) for axis in DP]
    rows = local.shape[0] // (sizes[0] * sizes[1] * sizes[2])
    joined = local.reshape(sizes[0], sizes[1], sizes[2], rows, width)
    for dim in (2, 1, 0):
        joined = lax.all_to_all(joined, DP[dim], dim, dim, tiled=True).sum(dim, keepdims=True)
    return joined.reshape(rows, width)


def embed(features, head):
    projected = jnp.dot(features, head, preferred_element_type=jnp.float32)
    inverse = lax.rsqrt(jnp.sum(projected * projected, axis=1) + EPSILON)
    unit = (projected * inverse[:, None]).astype(jnp.bfloat16)
    return projected, inverse, unit


def shards(image_feats, text_feats, image_head, text_head, hard_tiles, logit_scale, logit_bias):
    row_count = image_feats.shape[0]
    width_part = image_head.shape[1]
    per_block = row_count // 128
    model_count = lax.psum(1, "mp")
    model_index = lax.axis_index("mp")
    block_count = lax.psum(1, DP)
    share = row_count // model_count
    offsets = (-2, -1, 1, 2)
    slot_of_model = (0, 2, 1, 3)
    model_of_slot = tuple(slot_of_model.index(s) for s in range(4))
    pick_count = hard_tiles.shape[1] // len(offsets)
    temp_scale = logit_scale[0]
    shift_bias = logit_bias[0]

    pairs = []
    for block in range(block_count):
        for model in range(model_count):
            source = ((block + offsets[slot_of_model[model]]) % block_count) * model_count + model
            pairs.append((source, block * model_count + model))
    feats_near = lax.ppermute(text_feats, ALL, pairs)

    heads = lax.all_gather(jnp.stack([image_head, text_head]), "mp", axis=0, tiled=False)
    heads = jnp.transpose(heads, (1, 2, 0, 3)).reshape(2, image_head.shape[0], -1)
    head_img, head_txt = heads[0], heads[1]
    image_proj, inverse_img, image_unit = embed(image_feats, head_img)
    text_proj, inverse_txt, text_unit = embed(text_feats, head_txt)
    text_near = embed(feats_near, head_txt)[2]

    local_ids = hard_tiles % per_block
    my_slot = jnp.array(slot_of_model, jnp.int32)[model_index]
    my_picks = lax.dynamic_slice_in_dim(local_ids, my_slot * pick_count, pick_count, 1)
    image_tiles_full = image_unit.reshape(per_block, 128, image_unit.shape[1])
    near_tiles = text_near.reshape(per_block, 128, text_near.shape[1])
    chosen_full = jnp.take(near_tiles, my_picks, axis=0)
    pair_scores = jnp.einsum(
        "rpe,rkqe->rkpq", image_tiles_full, chosen_full, preferred_element_type=jnp.float32
    )
    hard_weight = (temp_scale * jax.nn.sigmoid(temp_scale * pair_scores + shift_bias)).astype(
        jnp.bfloat16
    )

    own_scores = jnp.dot(image_unit, text_unit.T, preferred_element_type=jnp.float32)
    diagonal_mask = jnp.eye(row_count, dtype=jnp.float32)
    weight = (
        temp_scale * (jax.nn.sigmoid(temp_scale * own_scores + shift_bias) - diagonal_mask)
    ).astype(jnp.bfloat16)

    hard_all = lax.all_gather(hard_weight, "mp", axis=0, tiled=False)

    text_split = text_near.reshape(row_count, model_count, width_part)
    text_split = lax.all_to_all(text_split, "mp", 1, 1, tiled=True)

    e_start = model_index * width_part
    text_local = lax.dynamic_slice_in_dim(text_unit, e_start, width_part, 1)
    image_local = lax.dynamic_slice_in_dim(image_unit, e_start, width_part, 1)
    proj_img = lax.dynamic_slice_in_dim(image_proj, e_start, width_part, 1)
    proj_txt = lax.dynamic_slice_in_dim(text_proj, e_start, width_part, 1)
    image_tiles = image_local.reshape(per_block, 128, width_part)

    grad_img = jnp.dot(weight, text_local, preferred_element_type=jnp.float32)
    grad_txt = jnp.einsum("pq,pe->qe", weight, image_local, preferred_element_type=jnp.float32)
    returned = []
    sends = []
    for slot, offset in enumerate(offsets):
        pair_weight = hard_all[model_of_slot[slot]]
        picked = local_ids[:, pick_count * slot : pick_count * slot + pick_count]
        into_sel = jnp.einsum(
            "rkpq,rpe->rkqe", pair_weight, image_tiles, preferred_element_type=jnp.float32
        )
        onehot = (
            picked[:, :, None] == jnp.arange(per_block, dtype=jnp.int32)[None, None, :]
        ).astype(jnp.float32)
        into_txt = jnp.einsum("rkt,rkqe->tqe", onehot, into_sel, precision=lax.Precision.HIGHEST)
        into_txt = into_txt.reshape(row_count, width_part)
        sends.append(into_txt)
        returned.append(shifted(into_txt, DP, offset))
    hard_all, text_split, _ = lax.optimization_barrier((hard_all, text_split, sends))
    for slot, offset in enumerate(offsets):
        source_model = model_of_slot[slot]
        pair_weight = hard_all[source_model]
        picked = local_ids[:, pick_count * slot : pick_count * slot + pick_count]
        near_local = text_split[:, source_model, :].reshape(per_block, 128, width_part)
        chosen = jnp.take(near_local, picked, axis=0)
        into_img = jnp.einsum(
            "rkpq,rkqe->rpe", pair_weight, chosen, preferred_element_type=jnp.float32
        )
        grad_img = grad_img + into_img.reshape(row_count, width_part)

    dots_img = lax.psum(jnp.sum(proj_img * grad_img, axis=1), "mp")
    local_img = head_part(image_feats, proj_img, inverse_img, grad_img, dots_img)
    out_img = reduce_rows(local_img)
    for part in returned:
        grad_txt = grad_txt + part
    dots_part = jnp.sum(proj_txt * grad_txt, axis=1)
    dots_img, dots_part = lax.optimization_barrier((dots_img, dots_part))
    dots_txt = lax.psum(dots_part, "mp")
    local_txt = head_part(text_feats, proj_txt, inverse_txt, grad_txt, dots_txt)
    return out_img, reduce_rows(local_txt)


def head_part(features, projected, inverse, grad, dots):
    cube = dots * inverse * inverse * inverse
    dproj = (inverse[:, None] * grad - cube[:, None] * projected).astype(jnp.bfloat16)
    return jnp.einsum("nd,ne->de", features, dproj, preferred_element_type=jnp.float32)


def solution(mesh):
    dp_size = mesh.shape["dp"]
    x_size = 4 if dp_size % 4 == 0 else 1
    y_size = 2 if dp_size % (2 * x_size) == 0 and dp_size > 2 * x_size else 1
    z_size = dp_size // (x_size * y_size)
    split_mesh = Mesh(
        mesh.devices.reshape(y_size, z_size, x_size, mesh.shape["mp"]), DP + ("mp",)
    )
    placed = (P(DP, None), P(DP, None), P(None, "mp"), P(None, "mp"), P(DP, None), P(), P())
    return jax.shard_map(
        shards,
        mesh=split_mesh,
        in_specs=placed,
        out_specs=(P(DP, "mp"), P(DP, "mp")),
        check_vma=False,
    )
```

```python
import jax
import jax.numpy as jnp
from jax import lax
from jax.sharding import Mesh, PartitionSpec as P

EPSILON = 1e-06
DP = ("yh", "z", "x")
ALL = DP + ("mp",)


def shifted(value, axis, steps):
    count = lax.psum(1, axis)
    pairs = [(source, (source + steps) % count) for source in range(count)]
    return lax.ppermute(value, axis, pairs)


def reduce_rows(local):
    width = local.shape[1]
    sizes = [lax.psum(1, axis) for axis in DP]
    rows = local.shape[0] // (sizes[0] * sizes[1] * sizes[2])
    joined = local.reshape(sizes[0], sizes[1], sizes[2], rows, width)
    for dim in (2, 1, 0):
        joined = lax.all_to_all(joined, DP[dim], dim, dim, tiled=True).sum(dim, keepdims=True)
    return joined.reshape(rows, width)


def embed(features, head):
    projected = jnp.dot(features, head, preferred_element_type=jnp.float32)
    inverse = lax.rsqrt(jnp.sum(projected * projected, axis=1) + EPSILON)
    unit = (projected * inverse[:, None]).astype(jnp.bfloat16)
    return projected, inverse, unit


def shards(image_feats, text_feats, image_head, text_head, hard_tiles, logit_scale, logit_bias):
    row_count = image_feats.shape[0]
    width_part = image_head.shape[1]
    per_block = row_count // 128
    model_count = lax.psum(1, "mp")
    model_index = lax.axis_index("mp")
    block_count = lax.psum(1, DP)
    share = row_count // model_count
    offsets = (-2, -1, 1, 2)
    slot_of_model = (0, 2, 1, 3)
    model_of_slot = tuple(slot_of_model.index(s) for s in range(4))
    pick_count = hard_tiles.shape[1] // len(offsets)
    temp_scale = logit_scale[0]
    shift_bias = logit_bias[0]

    pairs = []
    for block in range(block_count):
        for model in range(model_count):
            source = ((block + offsets[slot_of_model[model]]) % block_count) * model_count + model
            pairs.append((source, block * model_count + model))
    feats_near = lax.ppermute(text_feats, ALL, pairs)

    heads = lax.all_gather(jnp.stack([image_head, text_head]), "mp", axis=0, tiled=False)
    heads = jnp.transpose(heads, (1, 2, 0, 3)).reshape(2, image_head.shape[0], -1)
    head_img, head_txt = heads[0], heads[1]
    image_proj, inverse_img, image_unit = embed(image_feats, head_img)
    text_proj, inverse_txt, text_unit = embed(text_feats, head_txt)
    text_near = embed(feats_near, head_txt)[2]

    local_ids = hard_tiles % per_block
    my_slot = jnp.array(slot_of_model, jnp.int32)[model_index]
    my_picks = lax.dynamic_slice_in_dim(local_ids, my_slot * pick_count, pick_count, 1)
    image_tiles_full = image_unit.reshape(per_block, 128, image_unit.shape[1])
    near_tiles = text_near.reshape(per_block, 128, text_near.shape[1])
    chosen_full = jnp.take(near_tiles, my_picks, axis=0)
    pair_scores = jnp.einsum(
        "rpe,rkqe->rkpq", image_tiles_full, chosen_full, preferred_element_type=jnp.float32
    )
    hard_weight = (temp_scale * jax.nn.sigmoid(temp_scale * pair_scores + shift_bias)).astype(
        jnp.bfloat16
    )

    own_scores = jnp.dot(image_unit, text_unit.T, preferred_element_type=jnp.float32)
    diagonal_mask = jnp.eye(row_count, dtype=jnp.float32)
    weight = (
        temp_scale * (jax.nn.sigmoid(temp_scale * own_scores + shift_bias) - diagonal_mask)
    ).astype(jnp.bfloat16)

    hard_all = lax.all_gather(hard_weight, "mp", axis=0, tiled=False)

    text_split = text_near.reshape(row_count, model_count, width_part)
    text_split = lax.all_to_all(text_split, "mp", 1, 1, tiled=True)

    e_start = model_index * width_part
    text_local = lax.dynamic_slice_in_dim(text_unit, e_start, width_part, 1)
    image_local = lax.dynamic_slice_in_dim(image_unit, e_start, width_part, 1)
    proj_img = lax.dynamic_slice_in_dim(image_proj, e_start, width_part, 1)
    proj_txt = lax.dynamic_slice_in_dim(text_proj, e_start, width_part, 1)

    grad_img = jnp.dot(weight, text_local, preferred_element_type=jnp.float32)
    grad_txt = jnp.einsum("pq,pe->qe", weight, image_local, preferred_element_type=jnp.float32)
    returned = []
    for slot, offset in enumerate(offsets):
        source_model = model_of_slot[slot]
        picked = local_ids[:, pick_count * slot : pick_count * slot + pick_count]
        onehot = (
            picked[:, :, None] == jnp.arange(per_block, dtype=jnp.int32)[None, None, :]
        ).astype(jnp.bfloat16)
        spread = jnp.einsum(
            "rkt,rkpq->rptq", onehot, hard_all[source_model], preferred_element_type=jnp.float32
        )
        spread = spread.astype(jnp.bfloat16).reshape(row_count, row_count)
        into_txt = jnp.einsum(
            "pq,pe->qe", spread, image_local, preferred_element_type=jnp.float32
        )
        returned.append(shifted(into_txt, DP, offset))
        grad_img = grad_img + jnp.dot(
            spread, text_split[:, source_model, :], preferred_element_type=jnp.float32
        )

    dots_img = lax.psum(jnp.sum(proj_img * grad_img, axis=1), "mp")
    local_img = head_part(image_feats, proj_img, inverse_img, grad_img, dots_img)
    out_img = reduce_rows(local_img)
    for part in returned:
        grad_txt = grad_txt + part
    dots_part = jnp.sum(proj_txt * grad_txt, axis=1)
    dots_img, dots_part = lax.optimization_barrier((dots_img, dots_part))
    dots_txt = lax.psum(dots_part, "mp")
    local_txt = head_part(text_feats, proj_txt, inverse_txt, grad_txt, dots_txt)
    return out_img, reduce_rows(local_txt)


def head_part(features, projected, inverse, grad, dots):
    cube = dots * inverse * inverse * inverse
    dproj = (inverse[:, None] * grad - cube[:, None] * projected).astype(jnp.bfloat16)
    return jnp.einsum("nd,ne->de", features, dproj, preferred_element_type=jnp.float32)


def solution(mesh):
    dp_size = mesh.shape["dp"]
    x_size = 4 if dp_size % 4 == 0 else 1
    y_size = 2 if dp_size % (2 * x_size) == 0 and dp_size > 2 * x_size else 1
    z_size = dp_size // (x_size * y_size)
    split_mesh = Mesh(
        mesh.devices.reshape(y_size, z_size, x_size, mesh.shape["mp"]), DP + ("mp",)
    )
    placed = (P(DP, None), P(DP, None), P(None, "mp"), P(None, "mp"), P(DP, None), P(), P())
    return jax.shard_map(
        shards,
        mesh=split_mesh,
        in_specs=placed,
        out_specs=(P(DP, "mp"), P(DP, "mp")),
        check_vma=False,
    )
```

```python
import jax
import jax.numpy as jnp
from jax import lax
from jax.sharding import Mesh, PartitionSpec as P

EPSILON = 1e-06
DP = ("yh", "z", "x")
ALL = DP + ("mp",)


def shifted(value, axis, steps):
    count = lax.psum(1, axis)
    pairs = [(source, (source + steps) % count) for source in range(count)]
    return lax.ppermute(value, axis, pairs)


def reduce_rows(local):
    width = local.shape[1]
    sizes = [lax.psum(1, axis) for axis in DP]
    rows = local.shape[0] // (sizes[0] * sizes[1] * sizes[2])
    joined = local.reshape(sizes[0], sizes[1], sizes[2], rows, width)
    for dim in (2, 1, 0):
        joined = lax.all_to_all(joined, DP[dim], dim, dim, tiled=True).sum(dim, keepdims=True)
    return joined.reshape(rows, width)


def embed(features, head):
    projected = jnp.dot(features, head, preferred_element_type=jnp.float32)
    inverse = lax.rsqrt(jnp.sum(projected * projected, axis=1) + EPSILON)
    unit = (projected * inverse[:, None]).astype(jnp.bfloat16)
    return projected, inverse, unit


def shards(image_feats, text_feats, image_head, text_head, hard_tiles, logit_scale, logit_bias):
    row_count = image_feats.shape[0]
    width_part = image_head.shape[1]
    per_block = row_count // 128
    model_count = lax.psum(1, "mp")
    model_index = lax.axis_index("mp")
    block_count = lax.psum(1, DP)
    share = row_count // model_count
    offsets = (-2, -1, 1, 2)
    slot_of_model = (0, 2, 1, 3)
    model_of_slot = tuple(slot_of_model.index(s) for s in range(4))
    pick_count = hard_tiles.shape[1] // len(offsets)
    temp_scale = logit_scale[0]
    shift_bias = logit_bias[0]

    pairs = []
    for block in range(block_count):
        for model in range(model_count):
            source = ((block + offsets[slot_of_model[model]]) % block_count) * model_count + model
            pairs.append((source, block * model_count + model))
    feats_near = lax.ppermute(text_feats, ALL, pairs)

    heads = lax.all_gather(jnp.stack([image_head, text_head]), "mp", axis=0, tiled=False)
    heads = jnp.transpose(heads, (1, 2, 0, 3)).reshape(2, image_head.shape[0], -1)
    head_img, head_txt = heads[0], heads[1]
    image_proj, inverse_img, image_unit = embed(image_feats, head_img)
    text_proj, inverse_txt, text_unit = embed(text_feats, head_txt)
    text_near = embed(feats_near, head_txt)[2]

    local_ids = hard_tiles % per_block
    my_slot = jnp.array(slot_of_model, jnp.int32)[model_index]
    my_picks = lax.dynamic_slice_in_dim(local_ids, my_slot * pick_count, pick_count, 1)
    image_tiles_full = image_unit.reshape(per_block, 128, image_unit.shape[1])
    near_tiles = text_near.reshape(per_block, 128, text_near.shape[1])
    chosen_full = jnp.take(near_tiles, my_picks, axis=0)
    pair_scores = jnp.einsum(
        "rpe,rkqe->rkpq", image_tiles_full, chosen_full, preferred_element_type=jnp.float32
    )
    hard_weight = (temp_scale * jax.nn.sigmoid(temp_scale * pair_scores + shift_bias)).astype(
        jnp.bfloat16
    )

    own_scores = jnp.dot(image_unit, text_unit.T, preferred_element_type=jnp.float32)
    diagonal_mask = jnp.eye(row_count, dtype=jnp.float32)
    weight = (
        temp_scale * (jax.nn.sigmoid(temp_scale * own_scores + shift_bias) - diagonal_mask)
    ).astype(jnp.bfloat16)

    hard_all = lax.all_gather(hard_weight, "mp", axis=0, tiled=False)

    text_split = text_near.reshape(row_count, model_count, width_part)
    text_split = lax.all_to_all(text_split, "mp", 1, 1, tiled=True)

    e_start = model_index * width_part
    text_local = lax.dynamic_slice_in_dim(text_unit, e_start, width_part, 1)
    image_local = lax.dynamic_slice_in_dim(image_unit, e_start, width_part, 1)
    proj_img = lax.dynamic_slice_in_dim(image_proj, e_start, width_part, 1)
    proj_txt = lax.dynamic_slice_in_dim(text_proj, e_start, width_part, 1)

    grad_img = jnp.dot(weight, text_local, preferred_element_type=jnp.float32)
    grad_txt = jnp.einsum("pq,pe->qe", weight, image_local, preferred_element_type=jnp.float32)
    returned = []
    for slot, offset in enumerate(offsets):
        source_model = model_of_slot[slot]
        picked = local_ids[:, pick_count * slot : pick_count * slot + pick_count]
        onehot = (
            picked[:, :, None] == jnp.arange(per_block, dtype=jnp.int32)[None, None, :]
        ).astype(jnp.bfloat16)
        spread = jnp.einsum(
            "rkt,rkpq->rptq", onehot, hard_all[source_model], preferred_element_type=jnp.float32
        )
        spread = spread.astype(jnp.bfloat16).reshape(row_count, row_count)
        into_txt = jnp.einsum(
            "pq,pe->qe", spread, image_local, preferred_element_type=jnp.float32
        )
        returned.append(shifted(into_txt, DP, offset))
        grad_img = grad_img + jnp.dot(
            spread, text_split[:, source_model, :], preferred_element_type=jnp.float32
        )

    dots_img = lax.psum(jnp.sum(proj_img * grad_img, axis=1), "mp")
    local_img = head_part(image_feats, proj_img, inverse_img, grad_img, dots_img)
    out_img = reduce_rows(local_img)
    out_img, returned = lax.optimization_barrier((out_img, returned))
    for part in returned:
        grad_txt = grad_txt + part
    dots_part = jnp.sum(proj_txt * grad_txt, axis=1)
    dots_img, dots_part = lax.optimization_barrier((dots_img, dots_part))
    dots_txt = lax.psum(dots_part, "mp")
    local_txt = head_part(text_feats, proj_txt, inverse_txt, grad_txt, dots_txt)
    return out_img, reduce_rows(local_txt)


def head_part(features, projected, inverse, grad, dots):
    cube = dots * inverse * inverse * inverse
    dproj = (inverse[:, None] * grad - cube[:, None] * projected).astype(jnp.bfloat16)
    return jnp.einsum("nd,ne->de", features, dproj, preferred_element_type=jnp.float32)


def solution(mesh):
    dp_size = mesh.shape["dp"]
    x_size = 4 if dp_size % 4 == 0 else 1
    y_size = 2 if dp_size % (2 * x_size) == 0 and dp_size > 2 * x_size else 1
    z_size = dp_size // (x_size * y_size)
    split_mesh = Mesh(
        mesh.devices.reshape(y_size, z_size, x_size, mesh.shape["mp"]), DP + ("mp",)
    )
    placed = (P(DP, None), P(DP, None), P(None, "mp"), P(None, "mp"), P(DP, None), P(), P())
    return jax.shard_map(
        shards,
        mesh=split_mesh,
        in_specs=placed,
        out_specs=(P(DP, "mp"), P(DP, "mp")),
        check_vma=False,
    )
```

```python
import jax
import jax.numpy as jnp
from jax import lax
from jax.sharding import Mesh, PartitionSpec as P

EPSILON = 1e-06
DP = ("yh", "z", "x")
ALL = DP + ("mp",)


def shifted(value, axis, steps):
    count = lax.psum(1, axis)
    pairs = [(source, (source + steps) % count) for source in range(count)]
    return lax.ppermute(value, axis, pairs)


def reduce_rows(local):
    width = local.shape[1]
    sizes = [lax.psum(1, axis) for axis in DP]
    rows = local.shape[0] // (sizes[0] * sizes[1] * sizes[2])
    joined = local.reshape(sizes[0], sizes[1], sizes[2], rows, width)
    for dim in (2, 1, 0):
        joined = lax.all_to_all(joined, DP[dim], dim, dim, tiled=True).sum(dim, keepdims=True)
    return joined.reshape(rows, width)


def embed(features, head):
    projected = jnp.dot(features, head, preferred_element_type=jnp.float32)
    inverse = lax.rsqrt(jnp.sum(projected * projected, axis=1) + EPSILON)
    unit = (projected * inverse[:, None]).astype(jnp.bfloat16)
    return projected, inverse, unit


def shards(image_feats, text_feats, image_head, text_head, hard_tiles, logit_scale, logit_bias):
    row_count = image_feats.shape[0]
    width_part = image_head.shape[1]
    per_block = row_count // 128
    model_count = lax.psum(1, "mp")
    model_index = lax.axis_index("mp")
    block_count = lax.psum(1, DP)
    share = row_count // model_count
    offsets = (-2, -1, 1, 2)
    slot_of_model = (0, 2, 1, 3)
    model_of_slot = tuple(slot_of_model.index(s) for s in range(4))
    pick_count = hard_tiles.shape[1] // len(offsets)
    temp_scale = logit_scale[0]
    shift_bias = logit_bias[0]

    pairs = []
    for block in range(block_count):
        for model in range(model_count):
            source = ((block + offsets[slot_of_model[model]]) % block_count) * model_count + model
            pairs.append((source, block * model_count + model))
    feats_near = lax.ppermute(text_feats, ALL, pairs)

    heads = lax.all_gather(jnp.stack([image_head, text_head]), "mp", axis=0, tiled=False)
    heads = jnp.transpose(heads, (1, 2, 0, 3)).reshape(2, image_head.shape[0], -1)
    head_img, head_txt = heads[0], heads[1]
    image_proj, inverse_img, image_unit = embed(image_feats, head_img)
    text_near = embed(feats_near, head_txt)[2]

    local_ids = hard_tiles % per_block
    my_slot = jnp.array(slot_of_model, jnp.int32)[model_index]
    my_picks = lax.dynamic_slice_in_dim(local_ids, my_slot * pick_count, pick_count, 1)
    image_tiles_full = image_unit.reshape(per_block, 128, image_unit.shape[1])
    near_tiles = text_near.reshape(per_block, 128, text_near.shape[1])
    chosen_full = jnp.take(near_tiles, my_picks, axis=0)
    pair_scores = jnp.einsum(
        "rpe,rkqe->rkpq", image_tiles_full, chosen_full, preferred_element_type=jnp.float32
    )
    hard_weight = (temp_scale * jax.nn.sigmoid(temp_scale * pair_scores + shift_bias)).astype(
        jnp.bfloat16
    )

    hard_weight, own_feats = lax.optimization_barrier((hard_weight, text_feats))
    text_proj, inverse_txt, text_unit = embed(own_feats, head_txt)
    own_scores = jnp.dot(image_unit, text_unit.T, preferred_element_type=jnp.float32)
    diagonal_mask = jnp.eye(row_count, dtype=jnp.float32)
    weight = (
        temp_scale * (jax.nn.sigmoid(temp_scale * own_scores + shift_bias) - diagonal_mask)
    ).astype(jnp.bfloat16)

    hard_all = lax.all_gather(hard_weight, "mp", axis=0, tiled=False)

    text_split = text_near.reshape(row_count, model_count, width_part)
    text_split = lax.all_to_all(text_split, "mp", 1, 1, tiled=True)

    e_start = model_index * width_part
    text_local = lax.dynamic_slice_in_dim(text_unit, e_start, width_part, 1)
    image_local = lax.dynamic_slice_in_dim(image_unit, e_start, width_part, 1)
    proj_img = lax.dynamic_slice_in_dim(image_proj, e_start, width_part, 1)
    proj_txt = lax.dynamic_slice_in_dim(text_proj, e_start, width_part, 1)

    grad_img = jnp.dot(weight, text_local, preferred_element_type=jnp.float32)
    grad_txt = jnp.einsum("pq,pe->qe", weight, image_local, preferred_element_type=jnp.float32)
    returned = []
    for slot, offset in enumerate(offsets):
        source_model = model_of_slot[slot]
        picked = local_ids[:, pick_count * slot : pick_count * slot + pick_count]
        onehot = (
            picked[:, :, None] == jnp.arange(per_block, dtype=jnp.int32)[None, None, :]
        ).astype(jnp.bfloat16)
        spread = jnp.einsum(
            "rkt,rkpq->rptq", onehot, hard_all[source_model], preferred_element_type=jnp.float32
        )
        spread = spread.astype(jnp.bfloat16).reshape(row_count, row_count)
        into_txt = jnp.einsum(
            "pq,pe->qe", spread, image_local, preferred_element_type=jnp.float32
        )
        returned.append(shifted(into_txt, DP, offset))
        grad_img = grad_img + jnp.dot(
            spread, text_split[:, source_model, :], preferred_element_type=jnp.float32
        )

    dots_img = lax.psum(jnp.sum(proj_img * grad_img, axis=1), "mp")
    local_img = head_part(image_feats, proj_img, inverse_img, grad_img, dots_img)
    out_img = reduce_rows(local_img)
    for part in returned:
        grad_txt = grad_txt + part
    dots_part = jnp.sum(proj_txt * grad_txt, axis=1)
    dots_img, dots_part = lax.optimization_barrier((dots_img, dots_part))
    dots_txt = lax.psum(dots_part, "mp")
    local_txt = head_part(text_feats, proj_txt, inverse_txt, grad_txt, dots_txt)
    return out_img, reduce_rows(local_txt)


def head_part(features, projected, inverse, grad, dots):
    cube = dots * inverse * inverse * inverse
    dproj = (inverse[:, None] * grad - cube[:, None] * projected).astype(jnp.bfloat16)
    return jnp.einsum("nd,ne->de", features, dproj, preferred_element_type=jnp.float32)


def solution(mesh):
    dp_size = mesh.shape["dp"]
    x_size = 4 if dp_size % 4 == 0 else 1
    y_size = 2 if dp_size % (2 * x_size) == 0 and dp_size > 2 * x_size else 1
    z_size = dp_size // (x_size * y_size)
    split_mesh = Mesh(
        mesh.devices.reshape(y_size, z_size, x_size, mesh.shape["mp"]), DP + ("mp",)
    )
    placed = (P(DP, None), P(DP, None), P(None, "mp"), P(None, "mp"), P(DP, None), P(), P())
    return jax.shard_map(
        shards,
        mesh=split_mesh,
        in_specs=placed,
        out_specs=(P(DP, "mp"), P(DP, "mp")),
        check_vma=False,
    )
```

```python
import jax
import jax.numpy as jnp
from jax import lax
from jax.sharding import Mesh, PartitionSpec as P

EPSILON = 1e-06
DP = ("yh", "z", "x")
ALL = DP + ("mp",)


def shifted(value, axis, steps):
    count = lax.psum(1, axis)
    pairs = [(source, (source + steps) % count) for source in range(count)]
    return lax.ppermute(value, axis, pairs)


def stage(values, dim):
    values = lax.all_to_all(values, DP[dim], dim, dim, tiled=True)
    return values.sum(dim, keepdims=True)


def blocked(local):
    sizes = [lax.psum(1, axis) for axis in DP]
    rows = local.shape[0] // (sizes[0] * sizes[1] * sizes[2])
    return local.reshape(sizes[0], sizes[1], sizes[2], rows, local.shape[1])


def embed(features, head):
    projected = jnp.dot(features, head, preferred_element_type=jnp.float32)
    inverse = lax.rsqrt(jnp.sum(projected * projected, axis=1) + EPSILON)
    unit = (projected * inverse[:, None]).astype(jnp.bfloat16)
    return projected, inverse, unit


def shards(image_feats, text_feats, image_head, text_head, hard_tiles, logit_scale, logit_bias):
    row_count = image_feats.shape[0]
    width_part = image_head.shape[1]
    per_block = row_count // 128
    model_count = lax.psum(1, "mp")
    model_index = lax.axis_index("mp")
    block_count = lax.psum(1, DP)
    share = row_count // model_count
    offsets = (-2, -1, 1, 2)
    slot_of_model = (0, 2, 1, 3)
    model_of_slot = tuple(slot_of_model.index(s) for s in range(4))
    pick_count = hard_tiles.shape[1] // len(offsets)
    temp_scale = logit_scale[0]
    shift_bias = logit_bias[0]

    pairs = []
    for block in range(block_count):
        for model in range(model_count):
            source = ((block + offsets[slot_of_model[model]]) % block_count) * model_count + model
            pairs.append((source, block * model_count + model))
    feats_near = lax.ppermute(text_feats, ALL, pairs)

    heads = lax.all_gather(jnp.stack([image_head, text_head]), "mp", axis=0, tiled=False)
    heads = jnp.transpose(heads, (1, 2, 0, 3)).reshape(2, image_head.shape[0], -1)
    head_img, head_txt = heads[0], heads[1]
    image_proj, inverse_img, image_unit = embed(image_feats, head_img)
    text_proj, inverse_txt, text_unit = embed(text_feats, head_txt)
    text_near = embed(feats_near, head_txt)[2]

    local_ids = hard_tiles % per_block
    my_slot = jnp.array(slot_of_model, jnp.int32)[model_index]
    my_picks = lax.dynamic_slice_in_dim(local_ids, my_slot * pick_count, pick_count, 1)
    image_tiles_full = image_unit.reshape(per_block, 128, image_unit.shape[1])
    near_tiles = text_near.reshape(per_block, 128, text_near.shape[1])
    chosen_full = jnp.take(near_tiles, my_picks, axis=0)
    pair_scores = jnp.einsum(
        "rpe,rkqe->rkpq", image_tiles_full, chosen_full, preferred_element_type=jnp.float32
    )
    hard_weight = (temp_scale * jax.nn.sigmoid(temp_scale * pair_scores + shift_bias)).astype(
        jnp.bfloat16
    )

    own_scores = jnp.dot(image_unit, text_unit.T, preferred_element_type=jnp.float32)
    diagonal_mask = jnp.eye(row_count, dtype=jnp.float32)
    weight = (
        temp_scale * (jax.nn.sigmoid(temp_scale * own_scores + shift_bias) - diagonal_mask)
    ).astype(jnp.bfloat16)

    hard_all = lax.all_gather(hard_weight, "mp", axis=0, tiled=False)

    text_split = text_near.reshape(row_count, model_count, width_part)
    text_split = lax.all_to_all(text_split, "mp", 1, 1, tiled=True)

    e_start = model_index * width_part
    text_local = lax.dynamic_slice_in_dim(text_unit, e_start, width_part, 1)
    image_local = lax.dynamic_slice_in_dim(image_unit, e_start, width_part, 1)
    proj_img = lax.dynamic_slice_in_dim(image_proj, e_start, width_part, 1)
    proj_txt = lax.dynamic_slice_in_dim(text_proj, e_start, width_part, 1)

    grad_img = jnp.dot(weight, text_local, preferred_element_type=jnp.float32)
    grad_txt = jnp.einsum("pq,pe->qe", weight, image_local, preferred_element_type=jnp.float32)
    returned = []
    for slot, offset in enumerate(offsets):
        source_model = model_of_slot[slot]
        picked = local_ids[:, pick_count * slot : pick_count * slot + pick_count]
        onehot = (
            picked[:, :, None] == jnp.arange(per_block, dtype=jnp.int32)[None, None, :]
        ).astype(jnp.bfloat16)
        spread = jnp.einsum(
            "rkt,rkpq->rptq", onehot, hard_all[source_model], preferred_element_type=jnp.float32
        )
        spread = spread.astype(jnp.bfloat16).reshape(row_count, row_count)
        into_txt = jnp.einsum(
            "pq,pe->qe", spread, image_local, preferred_element_type=jnp.float32
        )
        returned.append(shifted(into_txt, DP, offset))
        grad_img = grad_img + jnp.dot(
            spread, text_split[:, source_model, :], preferred_element_type=jnp.float32
        )

    dots_img = lax.psum(jnp.sum(proj_img * grad_img, axis=1), "mp")
    local_img = head_part(image_feats, proj_img, inverse_img, grad_img, dots_img)
    part_img = stage(blocked(local_img), 2)
    for part in returned:
        grad_txt = grad_txt + part
    dots_part = jnp.sum(proj_txt * grad_txt, axis=1)
    dots_img, dots_part = lax.optimization_barrier((dots_img, dots_part))
    dots_txt = lax.psum(dots_part, "mp")
    local_txt = head_part(text_feats, proj_txt, inverse_txt, grad_txt, dots_txt)
    joined = jnp.concatenate([part_img, stage(blocked(local_txt), 2)], axis=-1)
    joined = stage(stage(joined, 1), 0)
    joined = joined.reshape(joined.shape[3], joined.shape[4])
    return joined[:, :width_part], joined[:, width_part:]


def head_part(features, projected, inverse, grad, dots):
    cube = dots * inverse * inverse * inverse
    dproj = (inverse[:, None] * grad - cube[:, None] * projected).astype(jnp.bfloat16)
    return jnp.einsum("nd,ne->de", features, dproj, preferred_element_type=jnp.float32)


def solution(mesh):
    dp_size = mesh.shape["dp"]
    x_size = 4 if dp_size % 4 == 0 else 1
    y_size = 2 if dp_size % (2 * x_size) == 0 and dp_size > 2 * x_size else 1
    z_size = dp_size // (x_size * y_size)
    split_mesh = Mesh(
        mesh.devices.reshape(y_size, z_size, x_size, mesh.shape["mp"]), DP + ("mp",)
    )
    placed = (P(DP, None), P(DP, None), P(None, "mp"), P(None, "mp"), P(DP, None), P(), P())
    return jax.shard_map(
        shards,
        mesh=split_mesh,
        in_specs=placed,
        out_specs=(P(DP, "mp"), P(DP, "mp")),
        check_vma=False,
    )
```

```python
import jax
import jax.numpy as jnp
from jax import lax
from jax.sharding import Mesh, PartitionSpec as P

EPSILON = 1e-06
DP = ("yh", "z", "x")
ALL = DP + ("mp",)


def shifted(value, axis, steps):
    count = lax.psum(1, axis)
    pairs = [(source, (source + steps) % count) for source in range(count)]
    return lax.ppermute(value, axis, pairs)


def stage(values, dim):
    values = lax.all_to_all(values, DP[dim], dim, dim, tiled=True)
    return values.sum(dim, keepdims=True)


def blocked(local):
    sizes = [lax.psum(1, axis) for axis in DP]
    rows = local.shape[0] // (sizes[0] * sizes[1] * sizes[2])
    return local.reshape(sizes[0], sizes[1], sizes[2], rows, local.shape[1])


def embed(features, head):
    projected = jnp.dot(features, head, preferred_element_type=jnp.float32)
    inverse = lax.rsqrt(jnp.sum(projected * projected, axis=1) + EPSILON)
    unit = (projected * inverse[:, None]).astype(jnp.bfloat16)
    return projected, inverse, unit


def shards(image_feats, text_feats, image_head, text_head, hard_tiles, logit_scale, logit_bias):
    row_count = image_feats.shape[0]
    width_part = image_head.shape[1]
    per_block = row_count // 128
    model_count = lax.psum(1, "mp")
    model_index = lax.axis_index("mp")
    block_count = lax.psum(1, DP)
    share = row_count // model_count
    offsets = (-2, -1, 1, 2)
    slot_of_model = (0, 2, 1, 3)
    model_of_slot = tuple(slot_of_model.index(s) for s in range(4))
    pick_count = hard_tiles.shape[1] // len(offsets)
    temp_scale = logit_scale[0]
    shift_bias = logit_bias[0]

    pairs = []
    for block in range(block_count):
        for model in range(model_count):
            source = ((block + offsets[slot_of_model[model]]) % block_count) * model_count + model
            pairs.append((source, block * model_count + model))
    feats_near = lax.ppermute(text_feats, ALL, pairs)

    heads = lax.all_gather(jnp.stack([image_head, text_head]), "mp", axis=0, tiled=False)
    heads = jnp.transpose(heads, (1, 2, 0, 3)).reshape(2, image_head.shape[0], -1)
    head_img, head_txt = heads[0], heads[1]
    image_proj, inverse_img, image_unit = embed(image_feats, head_img)
    text_proj, inverse_txt, text_unit = embed(text_feats, head_txt)
    text_near = embed(feats_near, head_txt)[2]

    local_ids = hard_tiles % per_block
    my_slot = jnp.array(slot_of_model, jnp.int32)[model_index]
    my_picks = lax.dynamic_slice_in_dim(local_ids, my_slot * pick_count, pick_count, 1)
    image_tiles_full = image_unit.reshape(per_block, 128, image_unit.shape[1])
    near_tiles = text_near.reshape(per_block, 128, text_near.shape[1])
    chosen_full = jnp.take(near_tiles, my_picks, axis=0)
    pair_scores = jnp.einsum(
        "rpe,rkqe->rkpq", image_tiles_full, chosen_full, preferred_element_type=jnp.float32
    )
    hard_weight = (temp_scale * jax.nn.sigmoid(temp_scale * pair_scores + shift_bias)).astype(
        jnp.bfloat16
    )

    own_scores = jnp.dot(image_unit, text_unit.T, preferred_element_type=jnp.float32)
    diagonal_mask = jnp.eye(row_count, dtype=jnp.float32)
    weight = (
        temp_scale * (jax.nn.sigmoid(temp_scale * own_scores + shift_bias) - diagonal_mask)
    ).astype(jnp.bfloat16)

    hard_all = lax.all_gather(hard_weight, "mp", axis=0, tiled=False)

    text_split = text_near.reshape(row_count, model_count, width_part)
    text_split = lax.all_to_all(text_split, "mp", 1, 1, tiled=True)

    e_start = model_index * width_part
    text_local = lax.dynamic_slice_in_dim(text_unit, e_start, width_part, 1)
    image_local = lax.dynamic_slice_in_dim(image_unit, e_start, width_part, 1)
    proj_img = lax.dynamic_slice_in_dim(image_proj, e_start, width_part, 1)
    proj_txt = lax.dynamic_slice_in_dim(text_proj, e_start, width_part, 1)

    grad_img = jnp.dot(weight, text_local, preferred_element_type=jnp.float32)
    grad_txt = jnp.einsum("pq,pe->qe", weight, image_local, preferred_element_type=jnp.float32)
    returned = []
    for slot, offset in enumerate(offsets):
        source_model = model_of_slot[slot]
        picked = local_ids[:, pick_count * slot : pick_count * slot + pick_count]
        onehot = (
            picked[:, :, None] == jnp.arange(per_block, dtype=jnp.int32)[None, None, :]
        ).astype(jnp.bfloat16)
        spread = jnp.einsum(
            "rkt,rkpq->rptq", onehot, hard_all[source_model], preferred_element_type=jnp.float32
        )
        spread = spread.astype(jnp.bfloat16).reshape(row_count, row_count)
        into_txt = jnp.einsum(
            "pq,pe->qe", spread, image_local, preferred_element_type=jnp.float32
        )
        returned.append(shifted(into_txt, DP, offset))
        grad_img = grad_img + jnp.dot(
            spread, text_split[:, source_model, :], preferred_element_type=jnp.float32
        )

    dots_img = lax.psum(jnp.sum(proj_img * grad_img, axis=1), "mp")
    local_img = head_part(image_feats, proj_img, inverse_img, grad_img, dots_img)
    part_img = stage(blocked(local_img), 2)
    for part in returned:
        grad_txt = grad_txt + part
    dots_part = jnp.sum(proj_txt * grad_txt, axis=1)
    dots_img, dots_part = lax.optimization_barrier((dots_img, dots_part))
    dots_txt = lax.psum(dots_part, "mp")
    cube = dots_txt * inverse_txt * inverse_txt * inverse_txt
    dproj_txt = (inverse_txt[:, None] * grad_txt - cube[:, None] * proj_txt).astype(jnp.bfloat16)
    feats_blocked = blocked(text_feats.T)
    local_txt = jnp.einsum(
        "abcrn,ne->abcre", feats_blocked, dproj_txt, preferred_element_type=jnp.float32
    )
    joined = jnp.concatenate([part_img, stage(local_txt, 2)], axis=-1)
    joined = stage(stage(joined, 1), 0)
    joined = joined.reshape(joined.shape[3], joined.shape[4])
    return joined[:, :width_part], joined[:, width_part:]


def head_part(features, projected, inverse, grad, dots):
    cube = dots * inverse * inverse * inverse
    dproj = (inverse[:, None] * grad - cube[:, None] * projected).astype(jnp.bfloat16)
    return jnp.einsum("nd,ne->de", features, dproj, preferred_element_type=jnp.float32)


def solution(mesh):
    dp_size = mesh.shape["dp"]
    x_size = 4 if dp_size % 4 == 0 else 1
    y_size = 2 if dp_size % (2 * x_size) == 0 and dp_size > 2 * x_size else 1
    z_size = dp_size // (x_size * y_size)
    split_mesh = Mesh(
        mesh.devices.reshape(y_size, z_size, x_size, mesh.shape["mp"]), DP + ("mp",)
    )
    placed = (P(DP, None), P(DP, None), P(None, "mp"), P(None, "mp"), P(DP, None), P(), P())
    return jax.shard_map(
        shards,
        mesh=split_mesh,
        in_specs=placed,
        out_specs=(P(DP, "mp"), P(DP, "mp")),
        check_vma=False,
    )
```

```python
import jax
import jax.numpy as jnp
from jax import lax
from jax.sharding import Mesh, PartitionSpec as P

EPSILON = 1e-06
DP = ("yh", "z", "x")
ALL = DP + ("mp",)


def shifted(value, axis, steps):
    count = lax.psum(1, axis)
    pairs = [(source, (source + steps) % count) for source in range(count)]
    return lax.ppermute(value, axis, pairs)


def stage(values, dim):
    values = lax.all_to_all(values, DP[dim], dim, dim, tiled=True)
    return values.sum(dim, keepdims=True)


def blocked(local):
    sizes = [lax.psum(1, axis) for axis in DP]
    rows = local.shape[0] // (sizes[0] * sizes[1] * sizes[2])
    return local.reshape(sizes[0], sizes[1], sizes[2], rows, local.shape[1])


def embed(features, head):
    projected = jnp.dot(features, head, preferred_element_type=jnp.float32)
    inverse = lax.rsqrt(jnp.sum(projected * projected, axis=1) + EPSILON)
    unit = (projected * inverse[:, None]).astype(jnp.bfloat16)
    return projected, inverse, unit


def shards(image_feats, text_feats, image_head, text_head, hard_tiles, logit_scale, logit_bias):
    row_count = image_feats.shape[0]
    width_part = image_head.shape[1]
    per_block = row_count // 128
    model_count = lax.psum(1, "mp")
    model_index = lax.axis_index("mp")
    block_count = lax.psum(1, DP)
    share = row_count // model_count
    offsets = (-2, -1, 1, 2)
    slot_of_model = (0, 2, 1, 3)
    model_of_slot = tuple(slot_of_model.index(s) for s in range(4))
    pick_count = hard_tiles.shape[1] // len(offsets)
    temp_scale = logit_scale[0]
    shift_bias = logit_bias[0]

    pairs = []
    for block in range(block_count):
        for model in range(model_count):
            source = ((block + offsets[slot_of_model[model]]) % block_count) * model_count + model
            pairs.append((source, block * model_count + model))
    feats_near = lax.ppermute(text_feats, ALL, pairs)

    heads = lax.all_gather(jnp.stack([image_head, text_head]), "mp", axis=0, tiled=False)
    heads = jnp.transpose(heads, (1, 2, 0, 3)).reshape(2, image_head.shape[0], -1)
    head_img, head_txt = heads[0], heads[1]
    image_proj, inverse_img, image_unit = embed(image_feats, head_img)
    text_proj, inverse_txt, text_unit = embed(text_feats, head_txt)
    text_near = embed(feats_near, head_txt)[2]

    local_ids = hard_tiles % per_block
    my_slot = jnp.array(slot_of_model, jnp.int32)[model_index]
    my_picks = lax.dynamic_slice_in_dim(local_ids, my_slot * pick_count, pick_count, 1)
    image_tiles_full = image_unit.reshape(per_block, 128, image_unit.shape[1])
    near_tiles = text_near.reshape(per_block, 128, text_near.shape[1])
    chosen_full = jnp.take(near_tiles, my_picks, axis=0)
    pair_scores = jnp.einsum(
        "rpe,rkqe->rkpq", image_tiles_full, chosen_full, preferred_element_type=jnp.float32
    )
    hard_weight = (temp_scale * jax.nn.sigmoid(temp_scale * pair_scores + shift_bias)).astype(
        jnp.bfloat16
    )

    own_scores = jnp.dot(image_unit, text_unit.T, preferred_element_type=jnp.float32)
    diagonal_mask = jnp.eye(row_count, dtype=jnp.float32)
    weight = (
        temp_scale * (jax.nn.sigmoid(temp_scale * own_scores + shift_bias) - diagonal_mask)
    ).astype(jnp.bfloat16)

    hard_all = lax.all_gather(hard_weight, "mp", axis=0, tiled=False)

    text_split = text_near.reshape(row_count, model_count, width_part)
    text_split = lax.all_to_all(text_split, "mp", 1, 1, tiled=True)

    e_start = model_index * width_part
    text_local = lax.dynamic_slice_in_dim(text_unit, e_start, width_part, 1)
    image_local = lax.dynamic_slice_in_dim(image_unit, e_start, width_part, 1)
    proj_img = lax.dynamic_slice_in_dim(image_proj, e_start, width_part, 1)
    proj_txt = lax.dynamic_slice_in_dim(text_proj, e_start, width_part, 1)

    grad_img = jnp.dot(weight, text_local, preferred_element_type=jnp.float32)
    grad_txt = jnp.einsum("pq,pe->qe", weight, image_local, preferred_element_type=jnp.float32)
    returned = []
    for slot, offset in enumerate(offsets):
        source_model = model_of_slot[slot]
        picked = local_ids[:, pick_count * slot : pick_count * slot + pick_count]
        onehot = (
            picked[:, :, None] == jnp.arange(per_block, dtype=jnp.int32)[None, None, :]
        ).astype(jnp.bfloat16)
        spread = jnp.einsum(
            "rkt,rkpq->rptq", onehot, hard_all[source_model], preferred_element_type=jnp.float32
        )
        spread = spread.astype(jnp.bfloat16).reshape(row_count, row_count)
        into_txt = jnp.einsum(
            "pq,pe->qe", spread, image_local, preferred_element_type=jnp.float32
        )
        returned.append(shifted(into_txt, DP, offset))
        grad_img = grad_img + jnp.dot(
            spread, text_split[:, source_model, :], preferred_element_type=jnp.float32
        )

    dots_img = lax.psum(jnp.sum(proj_img * grad_img, axis=1), "mp")
    cube_img = dots_img * inverse_img * inverse_img * inverse_img
    dproj_img = (inverse_img[:, None] * grad_img - cube_img[:, None] * proj_img).astype(jnp.bfloat16)
    local_img = jnp.einsum(
        "abcrn,ne->abcre", blocked(image_feats.T), dproj_img, preferred_element_type=jnp.float32
    )
    part_img = stage(local_img, 2)
    for part in returned:
        grad_txt = grad_txt + part
    dots_part = jnp.sum(proj_txt * grad_txt, axis=1)
    dots_img, dots_part = lax.optimization_barrier((dots_img, dots_part))
    dots_txt = lax.psum(dots_part, "mp")
    cube = dots_txt * inverse_txt * inverse_txt * inverse_txt
    dproj_txt = (inverse_txt[:, None] * grad_txt - cube[:, None] * proj_txt).astype(jnp.bfloat16)
    feats_blocked = blocked(text_feats.T)
    local_txt = jnp.einsum(
        "abcrn,ne->abcre", feats_blocked, dproj_txt, preferred_element_type=jnp.float32
    )
    joined = jnp.concatenate([part_img, stage(local_txt, 2)], axis=-1)
    joined = stage(stage(joined, 1), 0)
    joined = joined.reshape(joined.shape[3], joined.shape[4])
    return joined[:, :width_part], joined[:, width_part:]


def head_part(features, projected, inverse, grad, dots):
    cube = dots * inverse * inverse * inverse
    dproj = (inverse[:, None] * grad - cube[:, None] * projected).astype(jnp.bfloat16)
    return jnp.einsum("nd,ne->de", features, dproj, preferred_element_type=jnp.float32)


def solution(mesh):
    dp_size = mesh.shape["dp"]
    x_size = 4 if dp_size % 4 == 0 else 1
    y_size = 2 if dp_size % (2 * x_size) == 0 and dp_size > 2 * x_size else 1
    z_size = dp_size // (x_size * y_size)
    split_mesh = Mesh(
        mesh.devices.reshape(y_size, z_size, x_size, mesh.shape["mp"]), DP + ("mp",)
    )
    placed = (P(DP, None), P(DP, None), P(None, "mp"), P(None, "mp"), P(DP, None), P(), P())
    return jax.shard_map(
        shards,
        mesh=split_mesh,
        in_specs=placed,
        out_specs=(P(DP, "mp"), P(DP, "mp")),
        check_vma=False,
    )
```
